32 devices in a mesh: dp: 4 (over z), sp: 8 (over y, x, core).
Axes of the slice: x: 2, y: 2, z: 4, core: 2. Of those that a mesh axis runs over, the one named last changes fastest.
Arguments:
- tokens: bfloat16 [16384, 2048], P(('dp', 'sp')), may hold values from -64 to 64
- key_blocks: int32 [4, 64, 8], P('dp'), may hold values from 0 to 63, as said below
- key_count: int32 [4, 64], P('dp'), may hold values from 1 to 8
- w_query: bfloat16 [2048, 2048], P(('dp', 'sp')), may hold values from -0.25 to 0.25
- w_key: bfloat16 [2048, 512], P(('dp', 'sp')), may hold values from -0.125 to 0.125
- w_value: bfloat16 [2048, 512], P(('dp', 'sp')), may hold values from -0.125 to 0.125
- w_out: bfloat16 [2048, 2048], P(('dp', 'sp')), may hold values from -0.5 to 0.5
Outputs:
- projected: bfloat16 [16384, 2048], P(('dp', 'sp'))
The draws below stay inside these ranges and needn't reach their ends.
Inputs may be any that keep to these rules, and one draw needn't show every extreme that they name: `key_blocks`: the first key_count[d, b] slots of list (d, b) hold distinct key blocks of document d, none of them b - 1, b or b + 1: first those of the global blocks 0 to 1 that are not, then other blocks. Later slots hold blocks in range and carry no meaning.
All inputs are finite; a program needn't handle non-finite values.
Results may differ from the reference program's by a relative error of at most 0.012.
Values may be sent and summed in bfloat16 or wider, within the bound.
No kernel may reach another device: no remote copies, remote signals or barrier semaphores. Data moves between devices by JAX's collectives and lax.ppermute only.
A program may use at most 192 MiB of HBM per device.

```python
import jax
import jax.numpy as jnp
from jax import lax

D = 2048
HQ = 16
KV = 4
HD = 128
BS = 64
NG = 2
LS = 8
DOC = 4096
DOCS = 4


def block_lists(key):
    base = jax.random.fold_in(key, 101)
    key_drawn, key_number, key_place = jax.random.split(base, 3)
    blocks = DOC // BS
    query_block = jnp.arange(blocks, dtype=jnp.int32)[:, None]
    key_block = jnp.arange(blocks, dtype=jnp.int32)[None, :]
    within = jnp.abs(key_block - query_block) <= 1
    is_global = key_block < NG
    ranking = jnp.where(is_global & ~within, 0, jnp.where(~is_global & ~within, 1, 2)).astype(jnp.int32)
    drawn = jax.random.randint(key_drawn, (DOCS, blocks, blocks), 0, 1 << 20)
    scored = ranking[None] * (1 << 27) + drawn * blocks + key_block[None]
    ordered = jnp.argsort(scored, axis=-1, stable=True)[..., :LS].astype(jnp.int32)
    available = jnp.sum((is_global & ~within).astype(jnp.int32), axis=1)
    extra = jax.random.randint(key_number, (DOCS, blocks), 1, LS - NG + 1)
    forced = jax.random.randint(key_place, (DOCS, 1), NG + 2, blocks)
    extra = jnp.where(jnp.arange(blocks, dtype=jnp.int32)[None, :] == forced, LS - NG, extra)
    counts = (available[None, :] + extra).astype(jnp.int32)
    return (ordered, counts)


def draw_key_blocks(key, part):
    return block_lists(key)[0]


def draw_key_count(key, part):
    return block_lists(key)[1]


def draw_tokens(key, part):
    total_rows = DOCS * DOC
    key_base = jax.random.fold_in(key, 0)
    return jnp.clip(jax.random.normal(key_base, (total_rows, D), jnp.float32), -6.0, 6.0).astype(jnp.bfloat16)


def block_levels(key, shape, shards, least, top_value):
    def one(dim, parts):
        draws = jax.random.uniform(jax.random.fold_in(jax.random.fold_in(key, 6), dim), (parts,), jnp.float32, least / len(shards), top_value / len(shards))
        return jnp.repeat(jnp.exp(draws), shape[dim] // parts).reshape((-1,) + (1,) * (len(shape) - dim - 1))

    level = one(*shards[0])
    for cut in shards[1:]:
        level = level * one(*cut)
    return level


def noise(rng, shape, deviation, reach, cuts=(), kind=jnp.bfloat16):
    entries = jax.random.normal(rng, shape, jnp.float32) * deviation
    if len(cuts) > 0:
        entries = block_levels(rng, shape, cuts, -0.22, 0.18) * entries
    return jnp.clip(entries, min=-reach, max=reach).astype(kind)


def setup_inputs(seed: int = 0) -> dict:
    seeds = jax.random.split(jax.random.key(seed), 8)
    tokens = draw_tokens(jax.random.fold_in(seeds[7], 71), 0)
    key_blocks = draw_key_blocks(jax.random.fold_in(seeds[7], 71), 0)
    key_count = draw_key_count(jax.random.fold_in(seeds[7], 71), 0)
    w_query = noise(seeds[3], (D, HQ * HD), (D // 4) ** -0.5, 0.25, ((0, 32),))
    w_key = noise(seeds[4], (D, KV * HD), D ** -0.5, 0.125, ((0, 32),))
    w_value = noise(seeds[5], (D, KV * HD), D ** -0.5, 0.125, ((0, 32),))
    w_out = noise(seeds[6], (HQ * HD, D), HD ** -0.5, 0.5, ((0, 32),))
    return dict(tokens=tokens, key_blocks=key_blocks, key_count=key_count, w_query=w_query, w_key=w_key, w_value=w_value, w_out=w_out)


NEG_FILL = -1.0e30


def key_sets(block_ids, counts, first, blocks):
    count_rows = block_ids.shape[0]
    query_block = first + jnp.arange(count_rows, dtype=jnp.int32)
    near = query_block[:, None] + jnp.arange(-1, 2, dtype=jnp.int32)[None, :]
    near_ok = (near >= 0) & (near < blocks)
    slot_ok = jnp.arange(LS, dtype=jnp.int32)[None, :] < counts[:, None]
    chosen = jnp.concatenate([jnp.clip(near, 0, blocks - 1).astype(jnp.int32), block_ids.astype(jnp.int32)], axis=1)
    usable = jnp.concatenate([near_ok, slot_ok], axis=1)
    return chosen, usable


def softmax_rows(scores, axes):
    top = jnp.max(scores, axis=axes, keepdims=True)
    expo = jnp.exp(scores - top)
    return (expo / jnp.sum(expo, axis=axes, keepdims=True)).astype(jnp.bfloat16)


def attend_head(queries, keys, values, block_ids, counts):
    blocks = DOC // BS
    scale = HD ** -0.5
    query_blocks = queries.reshape(blocks, BS, HD).astype(jnp.float32)
    key_blocks = keys.reshape(blocks, BS, HD)
    value_blocks = values.reshape(blocks, BS, HD)
    chosen, usable = key_sets(block_ids, counts, 0, blocks)
    near_keys = key_blocks[chosen].astype(jnp.float32)
    near_values = value_blocks[chosen].astype(jnp.float32)
    scores = jnp.einsum("iqd,ijkd->iqjk", query_blocks, near_keys) * scale
    scores = jnp.where(usable[:, None, :, None], scores, NEG_FILL)
    weights = softmax_rows(scores, (2, 3))
    sparse = jnp.einsum("iqjk,ijkd->iqd", weights.astype(jnp.float32), near_values).reshape(DOC, HD)
    lead = NG * BS
    dense_scores = jnp.dot(queries[:lead], keys.T, preferred_element_type=jnp.float32) * scale
    dense_weights = softmax_rows(dense_scores, (1,))
    dense = jnp.dot(dense_weights, values, preferred_element_type=jnp.float32)
    return jnp.concatenate([dense, sparse[lead:]], axis=0).astype(jnp.bfloat16)


def reference(tokens, key_blocks, key_count, w_query, w_key, w_value, w_out):
    documents = tokens.shape[0] // DOC
    group = HQ // KV

    def one_document(packed):
        rows, block_ids, counts = packed
        queries = jnp.dot(rows, w_query, preferred_element_type=jnp.float32).astype(jnp.bfloat16).reshape(DOC, HQ, HD)
        keys = jnp.dot(rows, w_key, preferred_element_type=jnp.float32).astype(jnp.bfloat16).reshape(DOC, KV, HD)
        values = jnp.dot(rows, w_value, preferred_element_type=jnp.float32).astype(jnp.bfloat16).reshape(DOC, KV, HD)

        def one_head(head):
            shared = head // group
            query_one = lax.dynamic_index_in_dim(queries, head, 1, keepdims=False)
            key_one = lax.dynamic_index_in_dim(keys, shared, 1, keepdims=False)
            value_one = lax.dynamic_index_in_dim(values, shared, 1, keepdims=False)
            return attend_head(query_one, key_one, value_one, block_ids, counts)

        attended = lax.map(one_head, jnp.arange(HQ, dtype=jnp.int32))
        joined = jnp.transpose(attended, (1, 0, 2)).reshape(DOC, HQ * HD)
        return jnp.dot(joined, w_out, preferred_element_type=jnp.float32).astype(jnp.bfloat16)

    result = lax.map(one_document, (tokens.reshape(documents, DOC, D), key_blocks, key_count))
    return result.reshape(documents * DOC, D)
```

```python
import math

import jax
import jax.numpy as jnp
from jax import lax
from jax.sharding import PartitionSpec as P

HQ = 16
KV = 4
HD = 128
BS = 64
NG = 2
LS = 8
DOC = 4096


NEG_FILL = -1e30


def key_sets(block_ids, counts, first, blocks):
    count_rows = block_ids.shape[0]
    query_block = first + jnp.arange(count_rows, dtype=jnp.int32)
    near = query_block[:, None] + jnp.arange(-1, 2, dtype=jnp.int32)[None, :]
    near_ok = (near >= 0) & (near < blocks)
    slot_ok = jnp.arange(LS, dtype=jnp.int32)[None, :] < counts[:, None]
    chosen = jnp.concatenate([jnp.clip(near, 0, blocks - 1), block_ids], axis=1)
    usable = jnp.concatenate([near_ok, slot_ok], axis=1)
    return (chosen, usable)


def normalize(scores, axes):
    top = jnp.max(scores, axis=axes, keepdims=True)
    expo = jnp.exp(scores - top)
    return (expo / jnp.sum(expo, axis=axes, keepdims=True)).astype(jnp.bfloat16)


def sparse_block_rows(queries, first, keys, values, block_ids, counts):
    total = queries.shape[0] // BS
    heads = queries.shape[1]
    shared_heads = keys.shape[1]
    group = heads // shared_heads
    blocks = keys.shape[0] // BS
    stride = math.gcd(8, total)
    scale = HD ** (-0.5)
    key_blocks = keys.reshape(blocks, BS, shared_heads, HD)
    value_blocks = values.reshape(blocks, BS, shared_heads, HD)
    query_parts = queries.reshape(total // stride, stride, BS, shared_heads, group, HD)
    list_parts = block_ids.reshape(total // stride, stride, LS)
    count_parts = counts.reshape(total // stride, stride)
    starts = first + stride * jnp.arange(total // stride, dtype=jnp.int32)

    def one_part(packed):
        query_part, list_part, count_part, start = packed
        chosen, usable = key_sets(list_part, count_part, start, blocks)
        near_keys = key_blocks[chosen]
        near_values = value_blocks[chosen]
        scores = (
            jnp.einsum(
                "iqhgd,ijkhd->ihgqjk", query_part, near_keys, preferred_element_type=jnp.float32
            )
            * scale
        )
        scores = jnp.where(usable[:, None, None, None, :, None], scores, NEG_FILL)
        weights = normalize(scores, (4, 5))
        return jnp.einsum(
            "ihgqjk,ijkhd->iqhgd", weights, near_values, preferred_element_type=jnp.float32
        )

    attended = lax.map(one_part, (query_parts, list_parts, count_parts, starts))
    return attended.reshape(total * BS, heads, HD)


def dense_rows(queries, keys, values):
    count_rows = queries.shape[0]
    heads = queries.shape[1]
    shared_heads = keys.shape[1]
    group = heads // shared_heads
    scale = HD ** (-0.5)
    grouped = queries.reshape(count_rows, shared_heads, group, HD)
    scores = jnp.einsum("qhgd,khd->hgqk", grouped, keys, preferred_element_type=jnp.float32) * scale
    weights = normalize(scores, (3,))
    attended = jnp.einsum("hgqk,khd->qhgd", weights, values, preferred_element_type=jnp.float32)
    return attended.reshape(count_rows, heads, HD)


def gather_rows(w):
    return lax.all_gather(w, ("dp", "sp"), axis=0, tiled=True)


def per_device(tokens, key_blocks, key_count, w_query, w_key, w_value, w_out):
    count_rows = tokens.shape[0]
    kv_cols = w_key.shape[1]
    kv_weights = gather_rows(jnp.concatenate([w_key, w_value], axis=1))
    query_weights = gather_rows(w_query)
    kv_sum = jnp.dot(tokens, kv_weights, preferred_element_type=jnp.float32)
    query_sum = jnp.dot(tokens, query_weights, preferred_element_type=jnp.float32)
    queries = query_sum.astype(jnp.bfloat16).reshape(count_rows, HQ, HD)
    kv = kv_sum.astype(jnp.bfloat16).reshape(count_rows, 2, KV, HD)
    kv_all = lax.all_gather(kv, "sp", axis=0, tiled=True)
    key_all = kv_all[:, 0]
    value_all = kv_all[:, 1]
    offset = lax.axis_index("sp") * count_rows
    document = offset // DOC
    first = offset % DOC // BS
    list_doc = lax.dynamic_index_in_dim(key_blocks, document, 0, keepdims=False)
    count_doc = lax.dynamic_index_in_dim(key_count, document, 0, keepdims=False)
    list_rows = lax.dynamic_slice_in_dim(list_doc, first, count_rows // BS, 0)
    count_slice = lax.dynamic_slice_in_dim(count_doc, first, count_rows // BS, 0)
    sparse = sparse_block_rows(queries, first, key_all, value_all, list_rows, count_slice)
    lead = NG * BS
    head_rows = lax.cond(
        first == 0, lambda: dense_rows(queries[:lead], key_all, value_all), lambda: sparse[:lead]
    )
    merged = jnp.concatenate([head_rows, sparse[lead:]], axis=0).astype(jnp.bfloat16)
    joined = merged.reshape(count_rows, HQ * HD)
    output = jnp.dot(joined, gather_rows(w_out), preferred_element_type=jnp.float32)
    return output.astype(jnp.bfloat16)


def solution(mesh):
    in_specs = (
        P(("dp", "sp"), None),
        P("dp", None, None),
        P("dp", None),
        P(("dp", "sp"), None),
        P(("dp", "sp"), None),
        P(("dp", "sp"), None),
        P(("dp", "sp"), None),
    )
    out_specs = P(("dp", "sp"), None)
    return jax.shard_map(
        per_device, mesh=mesh, in_specs=in_specs, out_specs=out_specs, check_vma=False
    )
```

```python
import jax
import jax.numpy as jnp
from jax import lax
from jax.experimental import pallas as pl
from jax.experimental.pallas import tpu as pltpu
from jax.sharding import PartitionSpec as P

HQ = 16
KV = 4
HD = 128
BS = 64
NG = 2
LS = 8
SLOTS = 12
DOC = 4096


def attention_kernel(chosen_ref, usable_ref, dense_ref, q_ref, k_ref, v_ref, o_ref, ksel_ref, vsel_ref):
    qb = pl.program_id(1)
    group = q_ref.shape[1] // HD
    scale = HD ** (-0.5)
    q_all = jnp.concatenate([q_ref[:, g * HD:(g + 1) * HD] for g in range(group)], axis=0)

    def finish(scores, values):
        top = jnp.max(scores, axis=1, keepdims=True)
        expo = jnp.exp(scores - top)
        weights = (expo / jnp.sum(expo, axis=1, keepdims=True)).astype(jnp.bfloat16)
        out = jnp.dot(weights, values, preferred_element_type=jnp.float32).astype(o_ref.dtype)
        for g in range(group):
            o_ref[:, g * HD:(g + 1) * HD] = out[g * BS:(g + 1) * BS]

    @pl.when(dense_ref[qb] != 0)
    def _():
        scores = lax.dot_general(
            q_all, k_ref[...], (((1,), (1,)), ((), ())), preferred_element_type=jnp.float32
        ) * scale
        finish(scores, v_ref[...])

    @pl.when(dense_ref[qb] == 0)
    def _():
        for j in range(SLOTS):
            start = pl.multiple_of(chosen_ref[qb * SLOTS + j] * BS, BS)
            ksel_ref[j * BS:(j + 1) * BS, :] = k_ref[pl.ds(start, BS), :]
            vsel_ref[j * BS:(j + 1) * BS, :] = v_ref[pl.ds(start, BS), :]
        scores = lax.dot_general(
            q_all, ksel_ref[...], (((1,), (1,)), ((), ())), preferred_element_type=jnp.float32
        ) * scale
        slot = lax.broadcasted_iota(jnp.int32, (1, SLOTS * BS), 1) // BS
        keep = jnp.zeros((1, SLOTS * BS), jnp.bool_)
        for j in range(SLOTS):
            keep = keep | ((slot == j) & (usable_ref[qb * SLOTS + j] != 0))
        scores = jnp.where(keep, scores, -1e30)
        finish(scores, vsel_ref[...])


def block_attention(queries2d, kv2d, chosen, usable, dense):
    rows = queries2d.shape[0]
    nqb = rows // BS
    kv_heads = kv2d.shape[1] // (2 * HD)
    doc = kv2d.shape[0]
    width = queries2d.shape[1] // kv_heads
    grid_spec = pltpu.PrefetchScalarGridSpec(
        num_scalar_prefetch=3,
        grid=(kv_heads, nqb),
        in_specs=[
            pl.BlockSpec((BS, width), lambda h, b, *_: (b, h)),
            pl.BlockSpec((doc, HD), lambda h, b, *_: (0, h)),
            pl.BlockSpec((doc, HD), lambda h, b, *_: (0, kv_heads + h)),
        ],
        out_specs=pl.BlockSpec((BS, width), lambda h, b, *_: (b, h)),
        scratch_shapes=[pltpu.VMEM((SLOTS * BS, HD), jnp.bfloat16), pltpu.VMEM((SLOTS * BS, HD), jnp.bfloat16)],
    )
    return pl.pallas_call(
        attention_kernel,
        grid_spec=grid_spec,
        out_shape=jax.ShapeDtypeStruct(queries2d.shape, jnp.bfloat16),
    )(chosen.reshape(-1), usable.reshape(-1), dense, queries2d, kv2d, kv2d)


def slot_tables(block_ids, counts, first, blocks):
    nqb = block_ids.shape[0]
    query_block = first + jnp.arange(nqb, dtype=jnp.int32)
    near = query_block[:, None] + jnp.arange(-1, 2, dtype=jnp.int32)[None, :]
    near_ok = (near >= 0) & (near < blocks)
    slot_ok = jnp.arange(LS, dtype=jnp.int32)[None, :] < counts[:, None]
    pad = SLOTS - 3 - LS
    chosen = jnp.concatenate(
        [near, block_ids, jnp.broadcast_to(query_block[:, None], (nqb, pad))], axis=1
    )
    chosen = jnp.clip(chosen, 0, blocks - 1).astype(jnp.int32)
    usable = jnp.concatenate([near_ok, slot_ok, jnp.zeros((nqb, pad), jnp.bool_)], axis=1).astype(jnp.int32)
    dense = (query_block < NG).astype(jnp.int32)
    return chosen, usable, dense


def gather_rows(w):
    return lax.all_gather(w, ("dp", "sp"), axis=0, tiled=True)


def per_device(tokens, key_blocks, key_count, w_query, w_key, w_value, w_out):
    count_rows = tokens.shape[0]
    kv_weights = gather_rows(jnp.concatenate([w_key, w_value], axis=1))
    query_weights = gather_rows(w_query)
    kv_sum = jnp.dot(tokens, kv_weights, preferred_element_type=jnp.float32)
    query_sum = jnp.dot(tokens, query_weights, preferred_element_type=jnp.float32)
    queries = query_sum.astype(jnp.bfloat16)
    kv = kv_sum.astype(jnp.bfloat16)
    kv_all = lax.all_gather(kv, "sp", axis=0, tiled=True)
    offset = lax.axis_index("sp") * count_rows
    document = offset // DOC
    first = offset % DOC // BS
    blocks = kv_all.shape[0] // BS
    list_doc = lax.dynamic_index_in_dim(key_blocks, document, 0, keepdims=False)
    count_doc = lax.dynamic_index_in_dim(key_count, document, 0, keepdims=False)
    list_rows = lax.dynamic_slice_in_dim(list_doc, first, count_rows // BS, 0)
    count_slice = lax.dynamic_slice_in_dim(count_doc, first, count_rows // BS, 0)
    chosen, usable, dense = slot_tables(list_rows, count_slice, first, blocks)
    joined = block_attention(queries, kv_all, chosen, usable, dense)
    output = jnp.dot(joined, gather_rows(w_out), preferred_element_type=jnp.float32)
    return output.astype(jnp.bfloat16)


def solution(mesh):
    in_specs = (
        P(("dp", "sp"), None),
        P("dp", None, None),
        P("dp", None),
        P(("dp", "sp"), None),
        P(("dp", "sp"), None),
        P(("dp", "sp"), None),
        P(("dp", "sp"), None),
    )
    out_specs = P(("dp", "sp"), None)
    return jax.shard_map(
        per_device, mesh=mesh, in_specs=in_specs, out_specs=out_specs, check_vma=False
    )
```

```python
import functools

import jax
import jax.numpy as jnp
from jax import lax
from jax.experimental import pallas as pl
from jax.experimental.pallas import tpu as pltpu
from jax.sharding import PartitionSpec as P

HQ = 16
KV = 4
HD = 128
BS = 64
NG = 2
LS = 8
SLOTS = 12
DOC = 4096


def attention_kernel(chosen_ref, usable_ref, dense_ref, q_ref, k_ref, v_ref, o_ref, ksel_ref, vsel_ref):
    qb = pl.program_id(1)
    group = q_ref.shape[1] // HD
    scale = HD ** (-0.5)
    q_all = jnp.concatenate([q_ref[:, g * HD:(g + 1) * HD] for g in range(group)], axis=0)

    def finish(scores, values):
        top = jnp.max(scores, axis=1, keepdims=True)
        expo = jnp.exp(scores - top)
        weights = (expo / jnp.sum(expo, axis=1, keepdims=True)).astype(jnp.bfloat16)
        out = jnp.dot(weights, values, preferred_element_type=jnp.float32).astype(o_ref.dtype)
        for g in range(group):
            o_ref[:, g * HD:(g + 1) * HD] = out[g * BS:(g + 1) * BS]

    @pl.when(dense_ref[qb] != 0)
    def _():
        scores = lax.dot_general(
            q_all, k_ref[...], (((1,), (1,)), ((), ())), preferred_element_type=jnp.float32
        ) * scale
        finish(scores, v_ref[...])

    @pl.when(dense_ref[qb] == 0)
    def _():
        for j in range(SLOTS):
            start = pl.multiple_of(chosen_ref[qb * SLOTS + j] * BS, BS)
            ksel_ref[j * BS:(j + 1) * BS, :] = k_ref[pl.ds(start, BS), :]
            vsel_ref[j * BS:(j + 1) * BS, :] = v_ref[pl.ds(start, BS), :]
        scores = lax.dot_general(
            q_all, ksel_ref[...], (((1,), (1,)), ((), ())), preferred_element_type=jnp.float32
        ) * scale
        slot = lax.broadcasted_iota(jnp.int32, (1, SLOTS * BS), 1) // BS
        keep = jnp.zeros((1, SLOTS * BS), jnp.bool_)
        for j in range(SLOTS):
            keep = keep | ((slot == j) & (usable_ref[qb * SLOTS + j] != 0))
        scores = jnp.where(keep, scores, -1e30)
        finish(scores, vsel_ref[...])


def block_attention(queries2d, kv2d, chosen, usable, dense):
    rows = queries2d.shape[0]
    nqb = rows // BS
    kv_heads = kv2d.shape[1] // (2 * HD)
    doc = kv2d.shape[0]
    width = queries2d.shape[1] // kv_heads
    grid_spec = pltpu.PrefetchScalarGridSpec(
        num_scalar_prefetch=3,
        grid=(kv_heads, nqb),
        in_specs=[
            pl.BlockSpec((BS, width), lambda h, b, *_: (b, h)),
            pl.BlockSpec((doc, HD), lambda h, b, *_: (0, h)),
            pl.BlockSpec((doc, HD), lambda h, b, *_: (0, kv_heads + h)),
        ],
        out_specs=pl.BlockSpec((BS, width), lambda h, b, *_: (b, h)),
        scratch_shapes=[pltpu.VMEM((SLOTS * BS, HD), jnp.bfloat16), pltpu.VMEM((SLOTS * BS, HD), jnp.bfloat16)],
    )
    return pl.pallas_call(
        attention_kernel,
        grid_spec=grid_spec,
        out_shape=jax.ShapeDtypeStruct(queries2d.shape, jnp.bfloat16),
    )(chosen.reshape(-1), usable.reshape(-1), dense, queries2d, kv2d, kv2d)


def slot_tables(block_ids, counts, first, blocks):
    nqb = block_ids.shape[0]
    query_block = first + jnp.arange(nqb, dtype=jnp.int32)
    near = query_block[:, None] + jnp.arange(-1, 2, dtype=jnp.int32)[None, :]
    near_ok = (near >= 0) & (near < blocks)
    slot_ok = jnp.arange(LS, dtype=jnp.int32)[None, :] < counts[:, None]
    pad = SLOTS - 3 - LS
    chosen = jnp.concatenate(
        [near, block_ids, jnp.broadcast_to(query_block[:, None], (nqb, pad))], axis=1
    )
    chosen = jnp.clip(chosen, 0, blocks - 1).astype(jnp.int32)
    usable = jnp.concatenate([near_ok, slot_ok, jnp.zeros((nqb, pad), jnp.bool_)], axis=1).astype(jnp.int32)
    dense = (query_block < NG).astype(jnp.int32)
    return chosen, usable, dense


def ring_gather(block, axis, size):
    parts = [block]
    for shift in range(1, size):
        pairs = [(j, (j + shift) % size) for j in range(size)]
        parts.append(lax.ppermute(block, axis, pairs))
    return jnp.concatenate(parts, axis=0)


def remap_blocks(chosen, me, size, per_device):
    owner = chosen // per_device
    return ((me - owner) % size) * per_device + chosen % per_device


def gather_rows(w):
    return lax.all_gather(w, ("dp", "sp"), axis=0, tiled=True)


def per_device(sp_size, tokens, key_blocks, key_count, w_query, w_key, w_value, w_out):
    count_rows = tokens.shape[0]
    kv_weights = gather_rows(jnp.concatenate([w_key, w_value], axis=1))
    query_weights = gather_rows(w_query)
    kv_sum = jnp.dot(tokens, kv_weights, preferred_element_type=jnp.float32)
    query_sum = jnp.dot(tokens, query_weights, preferred_element_type=jnp.float32)
    queries = query_sum.astype(jnp.bfloat16)
    kv = kv_sum.astype(jnp.bfloat16)
    kv_all = ring_gather(kv, "sp", sp_size)
    me = lax.axis_index("sp")
    offset = me * count_rows
    document = offset // DOC
    first = offset % DOC // BS
    blocks = kv_all.shape[0] // BS
    list_doc = lax.dynamic_index_in_dim(key_blocks, document, 0, keepdims=False)
    count_doc = lax.dynamic_index_in_dim(key_count, document, 0, keepdims=False)
    list_rows = lax.dynamic_slice_in_dim(list_doc, first, count_rows // BS, 0)
    count_slice = lax.dynamic_slice_in_dim(count_doc, first, count_rows // BS, 0)
    chosen, usable, dense = slot_tables(list_rows, count_slice, first, blocks)
    chosen = remap_blocks(chosen, me, sp_size, count_rows // BS)
    joined = block_attention(queries, kv_all, chosen, usable, dense)
    output = jnp.dot(joined, gather_rows(w_out), preferred_element_type=jnp.float32)
    return output.astype(jnp.bfloat16)


def solution(mesh):
    in_specs = (
        P(("dp", "sp"), None),
        P("dp", None, None),
        P("dp", None),
        P(("dp", "sp"), None),
        P(("dp", "sp"), None),
        P(("dp", "sp"), None),
        P(("dp", "sp"), None),
    )
    out_specs = P(("dp", "sp"), None)
    return jax.shard_map(
        functools.partial(per_device, mesh.shape["sp"]), mesh=mesh, in_specs=in_specs, out_specs=out_specs, check_vma=False
    )
```

```python
import jax
import jax.numpy as jnp
from jax import lax
from jax.experimental import pallas as pl
from jax.experimental.pallas import tpu as pltpu
from jax.sharding import PartitionSpec as P

HQ = 16
KV = 4
HD = 128
BS = 64
NG = 2
LS = 8
SLOTS = 12
DOC = 4096


def attention_kernel(chosen_ref, usable_ref, dense_ref, q_ref, k_ref, v_ref, o_ref, ksel_ref, vsel_ref):
    qb = pl.program_id(1)
    group = q_ref.shape[1] // HD
    scale = HD ** (-0.5)
    q_all = jnp.concatenate([q_ref[:, g * HD:(g + 1) * HD] for g in range(group)], axis=0)

    def finish(scores, values):
        top = jnp.max(scores, axis=1, keepdims=True)
        expo = jnp.exp(scores - top)
        weights = (expo / jnp.sum(expo, axis=1, keepdims=True)).astype(jnp.bfloat16)
        out = jnp.dot(weights, values, preferred_element_type=jnp.float32).astype(o_ref.dtype)
        for g in range(group):
            o_ref[:, g * HD:(g + 1) * HD] = out[g * BS:(g + 1) * BS]

    @pl.when(dense_ref[qb] != 0)
    def _():
        scores = lax.dot_general(
            q_all, k_ref[...], (((1,), (1,)), ((), ())), preferred_element_type=jnp.float32
        ) * scale
        finish(scores, v_ref[...])

    @pl.when(dense_ref[qb] == 0)
    def _():
        for j in range(SLOTS):
            start = pl.multiple_of(chosen_ref[qb * SLOTS + j] * BS, BS)
            ksel_ref[j * BS:(j + 1) * BS, :] = k_ref[pl.ds(start, BS), :]
            vsel_ref[j * BS:(j + 1) * BS, :] = v_ref[pl.ds(start, BS), :]
        scores = lax.dot_general(
            q_all, ksel_ref[...], (((1,), (1,)), ((), ())), preferred_element_type=jnp.float32
        ) * scale
        slot = lax.broadcasted_iota(jnp.int32, (1, SLOTS * BS), 1) // BS
        keep = jnp.zeros((1, SLOTS * BS), jnp.bool_)
        for j in range(SLOTS):
            keep = keep | ((slot == j) & (usable_ref[qb * SLOTS + j] != 0))
        scores = jnp.where(keep, scores, -1e30)
        finish(scores, vsel_ref[...])


def block_attention(queries2d, kv2d, chosen, usable, dense):
    rows = queries2d.shape[0]
    nqb = rows // BS
    kv_heads = kv2d.shape[1] // (2 * HD)
    doc = kv2d.shape[0]
    width = queries2d.shape[1] // kv_heads
    grid_spec = pltpu.PrefetchScalarGridSpec(
        num_scalar_prefetch=3,
        grid=(kv_heads, nqb),
        in_specs=[
            pl.BlockSpec((BS, width), lambda h, b, *_: (b, h)),
            pl.BlockSpec((doc, HD), lambda h, b, *_: (0, h)),
            pl.BlockSpec((doc, HD), lambda h, b, *_: (0, kv_heads + h)),
        ],
        out_specs=pl.BlockSpec((BS, width), lambda h, b, *_: (b, h)),
        scratch_shapes=[pltpu.VMEM((SLOTS * BS, HD), jnp.bfloat16), pltpu.VMEM((SLOTS * BS, HD), jnp.bfloat16)],
    )
    return pl.pallas_call(
        attention_kernel,
        grid_spec=grid_spec,
        out_shape=jax.ShapeDtypeStruct(queries2d.shape, jnp.bfloat16),
    )(chosen.reshape(-1), usable.reshape(-1), dense, queries2d, kv2d, kv2d)


def slot_tables(block_ids, counts, first, blocks):
    nqb = block_ids.shape[0]
    query_block = first + jnp.arange(nqb, dtype=jnp.int32)
    near = query_block[:, None] + jnp.arange(-1, 2, dtype=jnp.int32)[None, :]
    near_ok = (near >= 0) & (near < blocks)
    slot_ok = jnp.arange(LS, dtype=jnp.int32)[None, :] < counts[:, None]
    pad = SLOTS - 3 - LS
    chosen = jnp.concatenate(
        [near, block_ids, jnp.broadcast_to(query_block[:, None], (nqb, pad))], axis=1
    )
    chosen = jnp.clip(chosen, 0, blocks - 1).astype(jnp.int32)
    usable = jnp.concatenate([near_ok, slot_ok, jnp.zeros((nqb, pad), jnp.bool_)], axis=1).astype(jnp.int32)
    dense = (query_block < NG).astype(jnp.int32)
    return chosen, usable, dense


def gather_rows(w):
    return lax.all_gather(w, ("dp", "sp"), axis=0, tiled=True)


def per_device(tokens, key_blocks, key_count, w_query, w_key, w_value, w_out):
    count_rows = tokens.shape[0]
    kv_cols = w_key.shape[1] + w_value.shape[1]
    q_cols = w_query.shape[1]
    weights = gather_rows(jnp.concatenate([w_key, w_value, w_query, w_out], axis=1))
    kv_sum = jnp.dot(tokens, weights[:, :kv_cols], preferred_element_type=jnp.float32)
    query_sum = jnp.dot(
        tokens, weights[:, kv_cols:kv_cols + q_cols], preferred_element_type=jnp.float32
    )
    queries = query_sum.astype(jnp.bfloat16)
    kv = kv_sum.astype(jnp.bfloat16)
    kv_all = lax.all_gather(kv, "sp", axis=0, tiled=True)
    offset = lax.axis_index("sp") * count_rows
    document = offset // DOC
    first = offset % DOC // BS
    blocks = kv_all.shape[0] // BS
    list_doc = lax.dynamic_index_in_dim(key_blocks, document, 0, keepdims=False)
    count_doc = lax.dynamic_index_in_dim(key_count, document, 0, keepdims=False)
    list_rows = lax.dynamic_slice_in_dim(list_doc, first, count_rows // BS, 0)
    count_slice = lax.dynamic_slice_in_dim(count_doc, first, count_rows // BS, 0)
    chosen, usable, dense = slot_tables(list_rows, count_slice, first, blocks)
    joined = block_attention(queries, kv_all, chosen, usable, dense)
    output = jnp.dot(joined, weights[:, kv_cols + q_cols:], preferred_element_type=jnp.float32)
    return output.astype(jnp.bfloat16)


def solution(mesh):
    in_specs = (
        P(("dp", "sp"), None),
        P("dp", None, None),
        P("dp", None),
        P(("dp", "sp"), None),
        P(("dp", "sp"), None),
        P(("dp", "sp"), None),
        P(("dp", "sp"), None),
    )
    out_specs = P(("dp", "sp"), None)
    return jax.shard_map(
        per_device, mesh=mesh, in_specs=in_specs, out_specs=out_specs, check_vma=False
    )
```

```python
import jax
import jax.numpy as jnp
from jax import lax
from jax.experimental import pallas as pl
from jax.experimental.pallas import tpu as pltpu
from jax.sharding import PartitionSpec as P

HQ = 16
KV = 4
HD = 128
BS = 64
NG = 2
LS = 8
SLOTS = 12
DOC = 4096


PAIR = 2


def attention_kernel(chosen_ref, usable_ref, dense_ref, q_ref, kv_ref, o_ref, sel_ref):
    step = pl.program_id(0)
    kv_heads = kv_ref.shape[1] // (2 * HD)
    group = q_ref.shape[1] // (kv_heads * HD)
    scale = HD ** (-0.5)

    def queries(h, rows):
        return jnp.concatenate(
            [q_ref[rows, (h * group + g) * HD:(h * group + g + 1) * HD] for g in range(group)], axis=0
        )

    def finish(h, scores, values, rows):
        top = jnp.max(scores, axis=1, keepdims=True)
        expo = jnp.exp(scores - top)
        weights = (expo / jnp.sum(expo, axis=1, keepdims=True)).astype(jnp.bfloat16)
        out = jnp.dot(weights, values, preferred_element_type=jnp.float32).astype(o_ref.dtype)
        n = rows.stop - rows.start
        for g in range(group):
            col = (h * group + g) * HD
            o_ref[rows, col:col + HD] = out[g * n:(g + 1) * n]

    def scores_of(h, keys, rows):
        return lax.dot_general(
            queries(h, rows), keys, (((1,), (1,)), ((), ())), preferred_element_type=jnp.float32
        ) * scale

    def sparse_block(qb, rows):
        for j in range(SLOTS):
            start = pl.multiple_of(chosen_ref[qb * SLOTS + j] * BS, BS)
            sel_ref[j * BS:(j + 1) * BS, :] = kv_ref[pl.ds(start, BS), :]
        slot = lax.broadcasted_iota(jnp.int32, (1, SLOTS * BS), 1) // BS
        keep = jnp.zeros((1, SLOTS * BS), jnp.bool_)
        for j in range(SLOTS):
            keep = keep | ((slot == j) & (usable_ref[qb * SLOTS + j] != 0))
        for h in range(kv_heads):
            keys = sel_ref[:, h * HD:(h + 1) * HD]
            values = sel_ref[:, (kv_heads + h) * HD:(kv_heads + h + 1) * HD]
            scores = jnp.where(keep, scores_of(h, keys, rows), -1e30)
            finish(h, scores, values, rows)

    @pl.when(dense_ref[step * PAIR] != 0)
    def _():
        rows = slice(0, PAIR * BS)
        for h in range(kv_heads):
            keys = kv_ref[:, h * HD:(h + 1) * HD]
            values = kv_ref[:, (kv_heads + h) * HD:(kv_heads + h + 1) * HD]
            finish(h, scores_of(h, keys, rows), values, rows)

    @pl.when(dense_ref[step * PAIR] == 0)
    def _():
        for half in range(PAIR):
            sparse_block(step * PAIR + half, slice(half * BS, (half + 1) * BS))


def block_attention(queries2d, kv2d, chosen, usable, dense):
    rows, width = queries2d.shape
    nqb = rows // BS
    grid_spec = pltpu.PrefetchScalarGridSpec(
        num_scalar_prefetch=3,
        grid=(nqb // PAIR,),
        in_specs=[
            pl.BlockSpec((PAIR * BS, width), lambda b, *_: (b, 0)),
            pl.BlockSpec(kv2d.shape, lambda b, *_: (0, 0), pipeline_mode=pl.Buffered(1)),
        ],
        out_specs=pl.BlockSpec((PAIR * BS, width), lambda b, *_: (b, 0)),
        scratch_shapes=[pltpu.VMEM((SLOTS * BS, kv2d.shape[1]), jnp.bfloat16)],
    )
    return pl.pallas_call(
        attention_kernel,
        grid_spec=grid_spec,
        out_shape=jax.ShapeDtypeStruct(queries2d.shape, jnp.bfloat16),
        compiler_params=pltpu.CompilerParams(vmem_limit_bytes=48 * 1024 * 1024),
    )(chosen.reshape(-1), usable.reshape(-1), dense, queries2d, kv2d)


def slot_tables(block_ids, counts, first, blocks):
    nqb = block_ids.shape[0]
    query_block = first + jnp.arange(nqb, dtype=jnp.int32)
    near = query_block[:, None] + jnp.arange(-1, 2, dtype=jnp.int32)[None, :]
    near_ok = (near >= 0) & (near < blocks)
    slot_ok = jnp.arange(LS, dtype=jnp.int32)[None, :] < counts[:, None]
    pad = SLOTS - 3 - LS
    chosen = jnp.concatenate(
        [near, block_ids, jnp.broadcast_to(query_block[:, None], (nqb, pad))], axis=1
    )
    chosen = jnp.clip(chosen, 0, blocks - 1).astype(jnp.int32)
    usable = jnp.concatenate([near_ok, slot_ok, jnp.zeros((nqb, pad), jnp.bool_)], axis=1).astype(jnp.int32)
    dense = (query_block < NG).astype(jnp.int32)
    return chosen, usable, dense


def gather_rows(w):
    return lax.all_gather(w, ("dp", "sp"), axis=0, tiled=True)


def per_device(tokens, key_blocks, key_count, w_query, w_key, w_value, w_out):
    count_rows = tokens.shape[0]
    kv_cols = w_key.shape[1] + w_value.shape[1]
    q_cols = w_query.shape[1]
    weights = gather_rows(jnp.concatenate([w_key, w_value, w_query, w_out], axis=1))
    kv_sum = jnp.dot(tokens, weights[:, :kv_cols], preferred_element_type=jnp.float32)
    query_sum = jnp.dot(
        tokens, weights[:, kv_cols:kv_cols + q_cols], preferred_element_type=jnp.float32
    )
    queries = query_sum.astype(jnp.bfloat16)
    kv = kv_sum.astype(jnp.bfloat16)
    kv_all = lax.all_gather(kv, "sp", axis=0, tiled=True)
    offset = lax.axis_index("sp") * count_rows
    document = offset // DOC
    first = offset % DOC // BS
    blocks = kv_all.shape[0] // BS
    list_doc = lax.dynamic_index_in_dim(key_blocks, document, 0, keepdims=False)
    count_doc = lax.dynamic_index_in_dim(key_count, document, 0, keepdims=False)
    list_rows = lax.dynamic_slice_in_dim(list_doc, first, count_rows // BS, 0)
    count_slice = lax.dynamic_slice_in_dim(count_doc, first, count_rows // BS, 0)
    chosen, usable, dense = slot_tables(list_rows, count_slice, first, blocks)
    joined = block_attention(queries, kv_all, chosen, usable, dense)
    output = jnp.dot(joined, weights[:, kv_cols + q_cols:], preferred_element_type=jnp.float32)
    return output.astype(jnp.bfloat16)


def solution(mesh):
    in_specs = (
        P(("dp", "sp"), None),
        P("dp", None, None),
        P("dp", None),
        P(("dp", "sp"), None),
        P(("dp", "sp"), None),
        P(("dp", "sp"), None),
        P(("dp", "sp"), None),
    )
    out_specs = P(("dp", "sp"), None)
    return jax.shard_map(
        per_device, mesh=mesh, in_specs=in_specs, out_specs=out_specs, check_vma=False
    )
```

```python
import functools

import jax
import jax.numpy as jnp
from jax import lax
from jax.experimental import pallas as pl
from jax.experimental.pallas import tpu as pltpu
from jax.sharding import PartitionSpec as P

HQ = 16
KV = 4
HD = 128
BS = 64
NG = 2
LS = 8
SLOTS = 12
DOC = 4096


PAIR = 2


def attention_kernel(chosen_ref, usable_ref, dense_ref, q_ref, kv_ref, o_ref, sel_ref):
    step = pl.program_id(0)
    kv_heads = kv_ref.shape[1] // (2 * HD)
    group = q_ref.shape[1] // (kv_heads * HD)
    scale = HD ** (-0.5)

    def queries(h, rows):
        return jnp.concatenate(
            [q_ref[rows, (h * group + g) * HD:(h * group + g + 1) * HD] for g in range(group)], axis=0
        )

    def finish(h, scores, values, rows):
        top = jnp.max(scores, axis=1, keepdims=True)
        expo = jnp.exp(scores - top)
        weights = (expo / jnp.sum(expo, axis=1, keepdims=True)).astype(jnp.bfloat16)
        out = jnp.dot(weights, values, preferred_element_type=jnp.float32).astype(o_ref.dtype)
        n = rows.stop - rows.start
        for g in range(group):
            col = (h * group + g) * HD
            o_ref[rows, col:col + HD] = out[g * n:(g + 1) * n]

    def scores_of(h, keys, rows):
        return lax.dot_general(
            queries(h, rows), keys, (((1,), (1,)), ((), ())), preferred_element_type=jnp.float32
        ) * scale

    def sparse_block(qb, rows):
        for j in range(SLOTS):
            start = pl.multiple_of(chosen_ref[qb * SLOTS + j] * BS, BS)
            sel_ref[j * BS:(j + 1) * BS, :] = kv_ref[pl.ds(start, BS), :]
        slot = lax.broadcasted_iota(jnp.int32, (1, SLOTS * BS), 1) // BS
        keep = jnp.zeros((1, SLOTS * BS), jnp.bool_)
        for j in range(SLOTS):
            keep = keep | ((slot == j) & (usable_ref[qb * SLOTS + j] != 0))
        for h in range(kv_heads):
            keys = sel_ref[:, h * HD:(h + 1) * HD]
            values = sel_ref[:, (kv_heads + h) * HD:(kv_heads + h + 1) * HD]
            scores = jnp.where(keep, scores_of(h, keys, rows), -1e30)
            finish(h, scores, values, rows)

    @pl.when(dense_ref[step * PAIR] == 0)
    def _():
        for half in range(PAIR):
            sparse_block(step * PAIR + half, slice(half * BS, (half + 1) * BS))


def block_attention(queries2d, kv2d, chosen, usable, dense):
    rows, width = queries2d.shape
    nqb = rows // BS
    grid_spec = pltpu.PrefetchScalarGridSpec(
        num_scalar_prefetch=3,
        grid=(nqb // PAIR,),
        in_specs=[
            pl.BlockSpec((PAIR * BS, width), lambda b, *_: (b, 0)),
            pl.BlockSpec(kv2d.shape, lambda b, *_: (0, 0), pipeline_mode=pl.Buffered(1)),
        ],
        out_specs=pl.BlockSpec((PAIR * BS, width), lambda b, *_: (b, 0)),
        scratch_shapes=[pltpu.VMEM((SLOTS * BS, kv2d.shape[1]), jnp.bfloat16)],
    )
    return pl.pallas_call(
        attention_kernel,
        grid_spec=grid_spec,
        out_shape=jax.ShapeDtypeStruct(queries2d.shape, jnp.bfloat16),
        compiler_params=pltpu.CompilerParams(vmem_limit_bytes=48 * 1024 * 1024),
    )(chosen.reshape(-1), usable.reshape(-1), dense, queries2d, kv2d)


def dense_kernel(head_ref, q_ref, k_ref, v_ref, o_ref):
    share = q_ref.shape[1] // HD
    rows = q_ref.shape[0]
    scale = HD ** (-0.5)
    q_all = jnp.concatenate([q_ref[:, g * HD:(g + 1) * HD] for g in range(share)], axis=0)
    scores = lax.dot_general(
        q_all, k_ref[...], (((1,), (1,)), ((), ())), preferred_element_type=jnp.float32
    ) * scale
    top = jnp.max(scores, axis=1, keepdims=True)
    expo = jnp.exp(scores - top)
    weights = (expo / jnp.sum(expo, axis=1, keepdims=True)).astype(jnp.bfloat16)
    out = jnp.dot(weights, v_ref[...], preferred_element_type=jnp.float32).astype(o_ref.dtype)
    for g in range(share):
        o_ref[:, g * HD:(g + 1) * HD] = out[g * rows:(g + 1) * rows]


def dense_share(q_share, kv2d, kv_head):
    doc = kv2d.shape[0]
    kv_heads = kv2d.shape[1] // (2 * HD)
    grid_spec = pltpu.PrefetchScalarGridSpec(
        num_scalar_prefetch=1,
        grid=(1,),
        in_specs=[
            pl.BlockSpec(q_share.shape, lambda i, hd: (0, 0)),
            pl.BlockSpec((doc, HD), lambda i, hd: (0, hd[0])),
            pl.BlockSpec((doc, HD), lambda i, hd: (0, kv_heads + hd[0])),
        ],
        out_specs=pl.BlockSpec(q_share.shape, lambda i, hd: (0, 0)),
    )
    return pl.pallas_call(
        dense_kernel,
        grid_spec=grid_spec,
        out_shape=jax.ShapeDtypeStruct(q_share.shape, jnp.bfloat16),
    )(kv_head, q_share, kv2d, kv2d)


def slot_tables(block_ids, counts, first, blocks):
    nqb = block_ids.shape[0]
    query_block = first + jnp.arange(nqb, dtype=jnp.int32)
    near = query_block[:, None] + jnp.arange(-1, 2, dtype=jnp.int32)[None, :]
    near_ok = (near >= 0) & (near < blocks)
    slot_ok = jnp.arange(LS, dtype=jnp.int32)[None, :] < counts[:, None]
    pad = SLOTS - 3 - LS
    chosen = jnp.concatenate(
        [near, block_ids, jnp.broadcast_to(query_block[:, None], (nqb, pad))], axis=1
    )
    chosen = jnp.clip(chosen, 0, blocks - 1).astype(jnp.int32)
    usable = jnp.concatenate([near_ok, slot_ok, jnp.zeros((nqb, pad), jnp.bool_)], axis=1).astype(jnp.int32)
    dense = (query_block < NG).astype(jnp.int32)
    return chosen, usable, dense


def gather_rows(w):
    return lax.all_gather(w, ("dp", "sp"), axis=0, tiled=True)


def per_device(sp_size, tokens, key_blocks, key_count, w_query, w_key, w_value, w_out):
    count_rows = tokens.shape[0]
    assert count_rows * sp_size == DOC and HQ % sp_size == 0
    kv_cols = w_key.shape[1] + w_value.shape[1]
    q_cols = w_query.shape[1]
    weights = gather_rows(jnp.concatenate([w_key, w_value, w_query, w_out], axis=1))
    kv_sum = jnp.dot(tokens, weights[:, :kv_cols], preferred_element_type=jnp.float32)
    query_sum = jnp.dot(
        tokens, weights[:, kv_cols:kv_cols + q_cols], preferred_element_type=jnp.float32
    )
    queries = query_sum.astype(jnp.bfloat16)
    kv = kv_sum.astype(jnp.bfloat16)
    kv_all = lax.all_gather(kv, "sp", axis=0, tiled=True)
    me = lax.axis_index("sp")
    offset = me * count_rows
    document = offset // DOC
    first = offset % DOC // BS
    blocks = kv_all.shape[0] // BS
    list_doc = lax.dynamic_index_in_dim(key_blocks, document, 0, keepdims=False)
    count_doc = lax.dynamic_index_in_dim(key_count, document, 0, keepdims=False)
    list_rows = lax.dynamic_slice_in_dim(list_doc, first, count_rows // BS, 0)
    count_slice = lax.dynamic_slice_in_dim(count_doc, first, count_rows // BS, 0)
    chosen, usable, dense = slot_tables(list_rows, count_slice, first, blocks)
    lead = NG * BS
    share_heads = HQ // sp_size
    share_cols = share_heads * HD
    q_lead = queries[:lead]
    q_share = jnp.where(me == 0, q_lead[:, :share_cols], jnp.zeros_like(q_lead[:, :share_cols]))
    for j in range(1, sp_size):
        piece = q_lead[:, j * share_cols:(j + 1) * share_cols]
        q_share = q_share + lax.ppermute(piece, "sp", [(0, j)])
    kv_head = ((me * share_heads) // (HQ // KV)).astype(jnp.int32)[None]
    out_share = dense_share(q_share, kv_all, kv_head)
    pieces = [out_share]
    for j in range(1, sp_size):
        pieces.append(lax.ppermute(out_share, "sp", [(j, 0)]))
    dense_rows = jnp.concatenate(pieces, axis=1)
    joined = block_attention(queries, kv_all, chosen, usable, dense)
    head = jnp.where(me == 0, dense_rows, joined[:lead])
    joined = jnp.concatenate([head, joined[lead:]], axis=0)
    output = jnp.dot(joined, weights[:, kv_cols + q_cols:], preferred_element_type=jnp.float32)
    return output.astype(jnp.bfloat16)


def solution(mesh):
    in_specs = (
        P(("dp", "sp"), None),
        P("dp", None, None),
        P("dp", None),
        P(("dp", "sp"), None),
        P(("dp", "sp"), None),
        P(("dp", "sp"), None),
        P(("dp", "sp"), None),
    )
    out_specs = P(("dp", "sp"), None)
    return jax.shard_map(
        functools.partial(per_device, mesh.shape["sp"]), mesh=mesh, in_specs=in_specs, out_specs=out_specs, check_vma=False
    )
```

```python
import functools

import jax
import jax.numpy as jnp
from jax import lax
from jax.experimental import pallas as pl
from jax.experimental.pallas import tpu as pltpu
from jax.sharding import PartitionSpec as P

HQ = 16
KV = 4
HD = 128
BS = 64
NG = 2
LS = 8
SLOTS = 12
DOC = 4096


PAIR = 2


def attention_kernel(chosen_ref, usable_ref, dense_ref, q_ref, kv_ref, o_ref, sel_ref):
    step = pl.program_id(0)
    kv_heads = kv_ref.shape[1] // (2 * HD)
    group = q_ref.shape[1] // (kv_heads * HD)
    scale = HD ** (-0.5)

    def queries(h, rows):
        return jnp.concatenate(
            [q_ref[rows, (h * group + g) * HD:(h * group + g + 1) * HD] for g in range(group)], axis=0
        )

    def finish(h, scores, values, rows):
        top = jnp.max(scores, axis=1, keepdims=True)
        expo = jnp.exp(scores - top)
        weights = (expo / jnp.sum(expo, axis=1, keepdims=True)).astype(jnp.bfloat16)
        out = jnp.dot(weights, values, preferred_element_type=jnp.float32).astype(o_ref.dtype)
        n = rows.stop - rows.start
        for g in range(group):
            col = (h * group + g) * HD
            o_ref[rows, col:col + HD] = out[g * n:(g + 1) * n]

    def scores_of(h, keys, rows):
        return lax.dot_general(
            queries(h, rows), keys, (((1,), (1,)), ((), ())), preferred_element_type=jnp.float32
        ) * scale

    def sparse_block(qb, rows):
        for j in range(SLOTS):
            start = pl.multiple_of(chosen_ref[qb * SLOTS + j] * BS, BS)
            sel_ref[j * BS:(j + 1) * BS, :] = kv_ref[pl.ds(start, BS), :]
        slot = lax.broadcasted_iota(jnp.int32, (1, SLOTS * BS), 1) // BS
        keep = jnp.zeros((1, SLOTS * BS), jnp.bool_)
        for j in range(SLOTS):
            keep = keep | ((slot == j) & (usable_ref[qb * SLOTS + j] != 0))
        for h in range(kv_heads):
            keys = sel_ref[:, h * HD:(h + 1) * HD]
            values = sel_ref[:, (kv_heads + h) * HD:(kv_heads + h + 1) * HD]
            scores = jnp.where(keep, scores_of(h, keys, rows), -1e30)
            finish(h, scores, values, rows)

    @pl.when(dense_ref[step * PAIR] == 0)
    def _():
        for half in range(PAIR):
            sparse_block(step * PAIR + half, slice(half * BS, (half + 1) * BS))


def block_attention(queries2d, kv2d, chosen, usable, dense):
    rows, width = queries2d.shape
    nqb = rows // BS
    grid_spec = pltpu.PrefetchScalarGridSpec(
        num_scalar_prefetch=3,
        grid=(nqb // PAIR,),
        in_specs=[
            pl.BlockSpec((PAIR * BS, width), lambda b, *_: (b, 0)),
            pl.BlockSpec(kv2d.shape, lambda b, *_: (0, 0), pipeline_mode=pl.Buffered(1)),
        ],
        out_specs=pl.BlockSpec((PAIR * BS, width), lambda b, *_: (b, 0)),
        scratch_shapes=[pltpu.VMEM((SLOTS * BS, kv2d.shape[1]), jnp.bfloat16)],
    )
    return pl.pallas_call(
        attention_kernel,
        grid_spec=grid_spec,
        out_shape=jax.ShapeDtypeStruct(queries2d.shape, jnp.bfloat16),
        compiler_params=pltpu.CompilerParams(vmem_limit_bytes=48 * 1024 * 1024),
    )(chosen.reshape(-1), usable.reshape(-1), dense, queries2d, kv2d)


def dense_kernel(head_ref, q_ref, k_ref, v_ref, o_ref):
    share = q_ref.shape[1] // HD
    rows = q_ref.shape[0]
    scale = HD ** (-0.5)
    q_all = jnp.concatenate([q_ref[:, g * HD:(g + 1) * HD] for g in range(share)], axis=0)
    scores = lax.dot_general(
        q_all, k_ref[...], (((1,), (1,)), ((), ())), preferred_element_type=jnp.float32
    ) * scale
    top = jnp.max(scores, axis=1, keepdims=True)
    expo = jnp.exp(scores - top)
    weights = (expo / jnp.sum(expo, axis=1, keepdims=True)).astype(jnp.bfloat16)
    out = jnp.dot(weights, v_ref[...], preferred_element_type=jnp.float32).astype(o_ref.dtype)
    for g in range(share):
        o_ref[:, g * HD:(g + 1) * HD] = out[g * rows:(g + 1) * rows]


def dense_share(q_share, kv2d, kv_head):
    doc = kv2d.shape[0]
    kv_heads = kv2d.shape[1] // (2 * HD)
    grid_spec = pltpu.PrefetchScalarGridSpec(
        num_scalar_prefetch=1,
        grid=(1,),
        in_specs=[
            pl.BlockSpec(q_share.shape, lambda i, hd: (0, 0)),
            pl.BlockSpec((doc, HD), lambda i, hd: (0, hd[0])),
            pl.BlockSpec((doc, HD), lambda i, hd: (0, kv_heads + hd[0])),
        ],
        out_specs=pl.BlockSpec(q_share.shape, lambda i, hd: (0, 0)),
    )
    return pl.pallas_call(
        dense_kernel,
        grid_spec=grid_spec,
        out_shape=jax.ShapeDtypeStruct(q_share.shape, jnp.bfloat16),
    )(kv_head, q_share, kv2d, kv2d)


def slot_tables(block_ids, counts, first, blocks):
    nqb = block_ids.shape[0]
    query_block = first + jnp.arange(nqb, dtype=jnp.int32)
    near = query_block[:, None] + jnp.arange(-1, 2, dtype=jnp.int32)[None, :]
    near_ok = (near >= 0) & (near < blocks)
    slot_ok = jnp.arange(LS, dtype=jnp.int32)[None, :] < counts[:, None]
    pad = SLOTS - 3 - LS
    chosen = jnp.concatenate(
        [near, block_ids, jnp.broadcast_to(query_block[:, None], (nqb, pad))], axis=1
    )
    chosen = jnp.clip(chosen, 0, blocks - 1).astype(jnp.int32)
    usable = jnp.concatenate([near_ok, slot_ok, jnp.zeros((nqb, pad), jnp.bool_)], axis=1).astype(jnp.int32)
    dense = (query_block < NG).astype(jnp.int32)
    return chosen, usable, dense


def gather_rows(w):
    return lax.all_gather(w, ("dp", "sp"), axis=0, tiled=True)


def per_device(sp_size, tokens, key_blocks, key_count, w_query, w_key, w_value, w_out):
    count_rows = tokens.shape[0]
    assert count_rows * sp_size == DOC and HQ % sp_size == 0
    kv_cols = w_key.shape[1] + w_value.shape[1]
    q_cols = w_query.shape[1]
    weights = gather_rows(jnp.concatenate([w_key, w_value, w_query, w_out], axis=1))
    kv_sum = jnp.dot(tokens, weights[:, :kv_cols], preferred_element_type=jnp.float32)
    query_sum = jnp.dot(
        tokens, weights[:, kv_cols:kv_cols + q_cols], preferred_element_type=jnp.float32
    )
    queries = query_sum.astype(jnp.bfloat16)
    kv = kv_sum.astype(jnp.bfloat16)
    kv_all = lax.all_gather(kv, "sp", axis=0, tiled=True)
    me = lax.axis_index("sp")
    offset = me * count_rows
    document = offset // DOC
    first = offset % DOC // BS
    blocks = kv_all.shape[0] // BS
    list_doc = lax.dynamic_index_in_dim(key_blocks, document, 0, keepdims=False)
    count_doc = lax.dynamic_index_in_dim(key_count, document, 0, keepdims=False)
    list_rows = lax.dynamic_slice_in_dim(list_doc, first, count_rows // BS, 0)
    count_slice = lax.dynamic_slice_in_dim(count_doc, first, count_rows // BS, 0)
    chosen, usable, dense = slot_tables(list_rows, count_slice, first, blocks)
    lead = NG * BS
    share_heads = HQ // sp_size
    share_cols = share_heads * HD
    q_lead = queries[:lead]
    q_share = jnp.where(me == 0, q_lead[:, :share_cols], jnp.zeros_like(q_lead[:, :share_cols]))
    for j in range(1, sp_size):
        piece = q_lead[:, j * share_cols:(j + 1) * share_cols]
        q_share = q_share + lax.ppermute(piece, "sp", [(0, j)])
    kv_head = ((me * share_heads) // (HQ // KV)).astype(jnp.int32)[None]
    out_share = dense_share(q_share, kv_all, kv_head)
    dense_rows = lax.all_gather(out_share, "sp", axis=1, tiled=True)
    joined = block_attention(queries, kv_all, chosen, usable, dense)
    head = jnp.where(me == 0, dense_rows, joined[:lead])
    joined = jnp.concatenate([head, joined[lead:]], axis=0)
    output = jnp.dot(joined, weights[:, kv_cols + q_cols:], preferred_element_type=jnp.float32)
    return output.astype(jnp.bfloat16)


def solution(mesh):
    in_specs = (
        P(("dp", "sp"), None),
        P("dp", None, None),
        P("dp", None),
        P(("dp", "sp"), None),
        P(("dp", "sp"), None),
        P(("dp", "sp"), None),
        P(("dp", "sp"), None),
    )
    out_specs = P(("dp", "sp"), None)
    return jax.shard_map(
        functools.partial(per_device, mesh.shape["sp"]), mesh=mesh, in_specs=in_specs, out_specs=out_specs, check_vma=False
    )
```

```python
import jax
import jax.numpy as jnp
from jax import lax
from jax.experimental import pallas as pl
from jax.experimental.pallas import tpu as pltpu
from jax.sharding import PartitionSpec as P

HQ = 16
KV = 4
HD = 128
BS = 64
NG = 2
LS = 8
SLOTS = 12
DOC = 4096


PAIR = 2
NARROW = 8


def attention_kernel(chosen_ref, usable_ref, dense_ref, valid_ref, q_ref, kv_ref, o_ref, sel_ref):
    step = pl.program_id(0)
    kv_heads = kv_ref.shape[1] // (2 * HD)
    group = q_ref.shape[1] // (kv_heads * HD)
    scale = HD ** (-0.5)

    def queries(h, rows):
        return jnp.concatenate(
            [q_ref[rows, (h * group + g) * HD:(h * group + g + 1) * HD] for g in range(group)], axis=0
        )

    def finish(h, scores, values, rows):
        top = jnp.max(scores, axis=1, keepdims=True)
        expo = jnp.exp(scores - top)
        weights = (expo / jnp.sum(expo, axis=1, keepdims=True)).astype(jnp.bfloat16)
        out = jnp.dot(weights, values, preferred_element_type=jnp.float32).astype(o_ref.dtype)
        n = rows.stop - rows.start
        for g in range(group):
            col = (h * group + g) * HD
            o_ref[rows, col:col + HD] = out[g * n:(g + 1) * n]

    def scores_of(h, keys, rows):
        return lax.dot_general(
            queries(h, rows), keys, (((1,), (1,)), ((), ())), preferred_element_type=jnp.float32
        ) * scale

    def sparse_width(qb, rows, slots):
        for j in range(slots):
            start = pl.multiple_of(chosen_ref[qb * SLOTS + j] * BS, BS)
            sel_ref[j * BS:(j + 1) * BS, :] = kv_ref[pl.ds(start, BS), :]
        slot = lax.broadcasted_iota(jnp.int32, (1, slots * BS), 1) // BS
        keep = jnp.zeros((1, slots * BS), jnp.bool_)
        for j in range(slots):
            keep = keep | ((slot == j) & (usable_ref[qb * SLOTS + j] != 0))
        for h in range(kv_heads):
            keys = sel_ref[0:slots * BS, h * HD:(h + 1) * HD]
            values = sel_ref[0:slots * BS, (kv_heads + h) * HD:(kv_heads + h + 1) * HD]
            scores = jnp.where(keep, scores_of(h, keys, rows), -1e30)
            finish(h, scores, values, rows)

    def sparse_block(qb, rows):
        @pl.when(valid_ref[qb] <= NARROW)
        def _():
            sparse_width(qb, rows, NARROW)

        @pl.when(valid_ref[qb] > NARROW)
        def _():
            sparse_width(qb, rows, SLOTS)

    @pl.when(dense_ref[step * PAIR] != 0)
    def _():
        rows = slice(0, PAIR * BS)
        for h in range(kv_heads):
            keys = kv_ref[:, h * HD:(h + 1) * HD]
            values = kv_ref[:, (kv_heads + h) * HD:(kv_heads + h + 1) * HD]
            finish(h, scores_of(h, keys, rows), values, rows)

    @pl.when(dense_ref[step * PAIR] == 0)
    def _():
        for half in range(PAIR):
            sparse_block(step * PAIR + half, slice(half * BS, (half + 1) * BS))


def block_attention(queries2d, kv2d, chosen, usable, dense, valid):
    rows, width = queries2d.shape
    nqb = rows // BS
    grid_spec = pltpu.PrefetchScalarGridSpec(
        num_scalar_prefetch=4,
        grid=(nqb // PAIR,),
        in_specs=[
            pl.BlockSpec((PAIR * BS, width), lambda b, *_: (b, 0)),
            pl.BlockSpec(kv2d.shape, lambda b, *_: (0, 0), pipeline_mode=pl.Buffered(1)),
        ],
        out_specs=pl.BlockSpec((PAIR * BS, width), lambda b, *_: (b, 0)),
        scratch_shapes=[pltpu.VMEM((SLOTS * BS, kv2d.shape[1]), jnp.bfloat16)],
    )
    return pl.pallas_call(
        attention_kernel,
        grid_spec=grid_spec,
        out_shape=jax.ShapeDtypeStruct(queries2d.shape, jnp.bfloat16),
        compiler_params=pltpu.CompilerParams(vmem_limit_bytes=48 * 1024 * 1024),
    )(chosen.reshape(-1), usable.reshape(-1), dense, valid, queries2d, kv2d)


def slot_tables(block_ids, counts, first, blocks):
    nqb = block_ids.shape[0]
    query_block = first + jnp.arange(nqb, dtype=jnp.int32)
    near = query_block[:, None] + jnp.arange(-1, 2, dtype=jnp.int32)[None, :]
    near_ok = (near >= 0) & (near < blocks)
    slot_ok = jnp.arange(LS, dtype=jnp.int32)[None, :] < counts[:, None]
    pad = SLOTS - 3 - LS
    chosen = jnp.concatenate(
        [near, block_ids, jnp.broadcast_to(query_block[:, None], (nqb, pad))], axis=1
    )
    chosen = jnp.clip(chosen, 0, blocks - 1).astype(jnp.int32)
    usable = jnp.concatenate([near_ok, slot_ok, jnp.zeros((nqb, pad), jnp.bool_)], axis=1).astype(jnp.int32)
    dense = (query_block < NG).astype(jnp.int32)
    order = jnp.argsort(1 - usable, axis=1, stable=True)
    chosen = jnp.take_along_axis(chosen, order, axis=1)
    usable = jnp.take_along_axis(usable, order, axis=1)
    valid = jnp.sum(usable, axis=1).astype(jnp.int32)
    return chosen, usable, dense, valid


def gather_rows(w):
    return lax.all_gather(w, ("dp", "sp"), axis=0, tiled=True)


def per_device(tokens, key_blocks, key_count, w_query, w_key, w_value, w_out):
    count_rows = tokens.shape[0]
    kv_cols = w_key.shape[1] + w_value.shape[1]
    q_cols = w_query.shape[1]
    weights = gather_rows(jnp.concatenate([w_key, w_value, w_query, w_out], axis=1))
    kv_sum = jnp.dot(tokens, weights[:, :kv_cols], preferred_element_type=jnp.float32)
    query_sum = jnp.dot(
        tokens, weights[:, kv_cols:kv_cols + q_cols], preferred_element_type=jnp.float32
    )
    queries = query_sum.astype(jnp.bfloat16)
    kv = kv_sum.astype(jnp.bfloat16)
    kv_all = lax.all_gather(kv, "sp", axis=0, tiled=True)
    offset = lax.axis_index("sp") * count_rows
    document = offset // DOC
    first = offset % DOC // BS
    blocks = kv_all.shape[0] // BS
    list_doc = lax.dynamic_index_in_dim(key_blocks, document, 0, keepdims=False)
    count_doc = lax.dynamic_index_in_dim(key_count, document, 0, keepdims=False)
    list_rows = lax.dynamic_slice_in_dim(list_doc, first, count_rows // BS, 0)
    count_slice = lax.dynamic_slice_in_dim(count_doc, first, count_rows // BS, 0)
    chosen, usable, dense, valid = slot_tables(list_rows, count_slice, first, blocks)
    joined = block_attention(queries, kv_all, chosen, usable, dense, valid)
    output = jnp.dot(joined, weights[:, kv_cols + q_cols:], preferred_element_type=jnp.float32)
    return output.astype(jnp.bfloat16)


def solution(mesh):
    in_specs = (
        P(("dp", "sp"), None),
        P("dp", None, None),
        P("dp", None),
        P(("dp", "sp"), None),
        P(("dp", "sp"), None),
        P(("dp", "sp"), None),
        P(("dp", "sp"), None),
    )
    out_specs = P(("dp", "sp"), None)
    return jax.shard_map(
        per_device, mesh=mesh, in_specs=in_specs, out_specs=out_specs, check_vma=False
    )
```

```python
import jax
import jax.numpy as jnp
from jax import lax
from jax.experimental import pallas as pl
from jax.experimental.pallas import tpu as pltpu
from jax.sharding import PartitionSpec as P

HQ = 16
KV = 4
HD = 128
BS = 64
NG = 2
LS = 8
SLOTS = 12
DOC = 4096


PAIR = 2


def attention_kernel(chosen_ref, usable_ref, dense_ref, q_ref, kv_ref, o_ref, sel_ref):
    step = pl.program_id(0)
    kv_heads = kv_ref.shape[1] // (2 * HD)
    group = q_ref.shape[1] // (kv_heads * HD)
    scale = HD ** (-0.5)

    def queries(h, rows):
        return jnp.concatenate(
            [q_ref[rows, (h * group + g) * HD:(h * group + g + 1) * HD] for g in range(group)], axis=0
        )

    def finish(h, scores, values, rows):
        top = jnp.max(scores, axis=1, keepdims=True)
        expo = jnp.exp(scores - top)
        weights = (expo / jnp.sum(expo, axis=1, keepdims=True)).astype(jnp.bfloat16)
        out = jnp.dot(weights, values, preferred_element_type=jnp.float32).astype(o_ref.dtype)
        n = rows.stop - rows.start
        for g in range(group):
            col = (h * group + g) * HD
            o_ref[rows, col:col + HD] = out[g * n:(g + 1) * n]

    def scores_of(h, keys, rows):
        return lax.dot_general(
            queries(h, rows), keys, (((1,), (1,)), ((), ())), preferred_element_type=jnp.float32
        ) * scale

    def sparse_block(qb, rows):
        for j in range(SLOTS):
            start = pl.multiple_of(chosen_ref[qb * SLOTS + j] * BS, BS)
            sel_ref[j * BS:(j + 1) * BS, :] = kv_ref[pl.ds(start, BS), :]
        slot = lax.broadcasted_iota(jnp.int32, (1, SLOTS * BS), 1) // BS
        keep = jnp.zeros((1, SLOTS * BS), jnp.bool_)
        for j in range(SLOTS):
            keep = keep | ((slot == j) & (usable_ref[qb * SLOTS + j] != 0))
        for h in range(kv_heads):
            keys = sel_ref[:, h * HD:(h + 1) * HD]
            values = sel_ref[:, (kv_heads + h) * HD:(kv_heads + h + 1) * HD]
            scores = jnp.where(keep, scores_of(h, keys, rows), -1e30)
            finish(h, scores, values, rows)

    @pl.when(dense_ref[step * PAIR] != 0)
    def _():
        rows = slice(0, PAIR * BS)
        for h in range(kv_heads // 2):
            keys = kv_ref[:, h * HD:(h + 1) * HD]
            values = kv_ref[:, (kv_heads + h) * HD:(kv_heads + h + 1) * HD]
            finish(h, scores_of(h, keys, rows), values, rows)

    @pl.when(dense_ref[step * PAIR] == 0)
    def _():
        for half in range(PAIR):
            sparse_block(step * PAIR + half, slice(half * BS, (half + 1) * BS))


def block_attention(queries2d, kv2d, chosen, usable, dense):
    rows, width = queries2d.shape
    nqb = rows // BS
    grid_spec = pltpu.PrefetchScalarGridSpec(
        num_scalar_prefetch=3,
        grid=(nqb // PAIR,),
        in_specs=[
            pl.BlockSpec((PAIR * BS, width), lambda b, *_: (b, 0)),
            pl.BlockSpec(kv2d.shape, lambda b, *_: (0, 0), pipeline_mode=pl.Buffered(1)),
        ],
        out_specs=pl.BlockSpec((PAIR * BS, width), lambda b, *_: (b, 0)),
        scratch_shapes=[pltpu.VMEM((SLOTS * BS, kv2d.shape[1]), jnp.bfloat16)],
    )
    return pl.pallas_call(
        attention_kernel,
        grid_spec=grid_spec,
        out_shape=jax.ShapeDtypeStruct(queries2d.shape, jnp.bfloat16),
        compiler_params=pltpu.CompilerParams(vmem_limit_bytes=48 * 1024 * 1024),
    )(chosen.reshape(-1), usable.reshape(-1), dense, queries2d, kv2d)


def far_kernel(q_ref, k_ref, v_ref, o_ref):
    group = q_ref.shape[1] // HD
    rows = q_ref.shape[0]
    scale = HD ** (-0.5)
    q_all = jnp.concatenate([q_ref[:, g * HD:(g + 1) * HD] for g in range(group)], axis=0)
    scores = lax.dot_general(
        q_all, k_ref[...], (((1,), (1,)), ((), ())), preferred_element_type=jnp.float32
    ) * scale
    top = jnp.max(scores, axis=1, keepdims=True)
    expo = jnp.exp(scores - top)
    weights = (expo / jnp.sum(expo, axis=1, keepdims=True)).astype(jnp.bfloat16)
    out = jnp.dot(weights, v_ref[...], preferred_element_type=jnp.float32).astype(o_ref.dtype)
    for g in range(group):
        o_ref[:, g * HD:(g + 1) * HD] = out[g * rows:(g + 1) * rows]


def far_heads(q_far, kv2d):
    doc = kv2d.shape[0]
    kv_heads = kv2d.shape[1] // (2 * HD)
    near = kv_heads // 2
    width = q_far.shape[1] // (kv_heads - near)
    return pl.pallas_call(
        far_kernel,
        grid=(kv_heads - near,),
        in_specs=[
            pl.BlockSpec((q_far.shape[0], width), lambda i: (0, i)),
            pl.BlockSpec((doc, HD), lambda i: (0, near + i)),
            pl.BlockSpec((doc, HD), lambda i: (0, kv_heads + near + i)),
        ],
        out_specs=pl.BlockSpec((q_far.shape[0], width), lambda i: (0, i)),
        out_shape=jax.ShapeDtypeStruct(q_far.shape, jnp.bfloat16),
    )(q_far, kv2d, kv2d)


def slot_tables(block_ids, counts, first, blocks):
    nqb = block_ids.shape[0]
    query_block = first + jnp.arange(nqb, dtype=jnp.int32)
    near = query_block[:, None] + jnp.arange(-1, 2, dtype=jnp.int32)[None, :]
    near_ok = (near >= 0) & (near < blocks)
    slot_ok = jnp.arange(LS, dtype=jnp.int32)[None, :] < counts[:, None]
    pad = SLOTS - 3 - LS
    chosen = jnp.concatenate(
        [near, block_ids, jnp.broadcast_to(query_block[:, None], (nqb, pad))], axis=1
    )
    chosen = jnp.clip(chosen, 0, blocks - 1).astype(jnp.int32)
    usable = jnp.concatenate([near_ok, slot_ok, jnp.zeros((nqb, pad), jnp.bool_)], axis=1).astype(jnp.int32)
    dense = (query_block < NG).astype(jnp.int32)
    return chosen, usable, dense


def gather_rows(w):
    return lax.all_gather(w, ("dp", "sp"), axis=0, tiled=True)


def per_device(tokens, key_blocks, key_count, w_query, w_key, w_value, w_out):
    count_rows = tokens.shape[0]
    kv_cols = w_key.shape[1] + w_value.shape[1]
    q_cols = w_query.shape[1]
    weights = gather_rows(jnp.concatenate([w_key, w_value, w_query, w_out], axis=1))
    kv_sum = jnp.dot(tokens, weights[:, :kv_cols], preferred_element_type=jnp.float32)
    query_sum = jnp.dot(
        tokens, weights[:, kv_cols:kv_cols + q_cols], preferred_element_type=jnp.float32
    )
    queries = query_sum.astype(jnp.bfloat16)
    kv = kv_sum.astype(jnp.bfloat16)
    kv_all = lax.all_gather(kv, "sp", axis=0, tiled=True)
    offset = lax.axis_index("sp") * count_rows
    document = offset // DOC
    first = offset % DOC // BS
    blocks = kv_all.shape[0] // BS
    list_doc = lax.dynamic_index_in_dim(key_blocks, document, 0, keepdims=False)
    count_doc = lax.dynamic_index_in_dim(key_count, document, 0, keepdims=False)
    list_rows = lax.dynamic_slice_in_dim(list_doc, first, count_rows // BS, 0)
    count_slice = lax.dynamic_slice_in_dim(count_doc, first, count_rows // BS, 0)
    chosen, usable, dense = slot_tables(list_rows, count_slice, first, blocks)
    lead = NG * BS
    half = queries.shape[1] // 2
    me = lax.axis_index("sp")
    q_far = lax.ppermute(queries[:lead, half:], "sp", [(0, 1)])
    out_far = lax.cond(
        me == 1, lambda: far_heads(q_far, kv_all), lambda: jnp.zeros_like(q_far)
    )
    back = lax.ppermute(out_far, "sp", [(1, 0)])
    joined = block_attention(queries, kv_all, chosen, usable, dense)
    dense_rows = jnp.concatenate([joined[:lead, :half], back], axis=1)
    head = jnp.where(me == 0, dense_rows, joined[:lead])
    joined = jnp.concatenate([head, joined[lead:]], axis=0)
    output = jnp.dot(joined, weights[:, kv_cols + q_cols:], preferred_element_type=jnp.float32)
    return output.astype(jnp.bfloat16)


def solution(mesh):
    in_specs = (
        P(("dp", "sp"), None),
        P("dp", None, None),
        P("dp", None),
        P(("dp", "sp"), None),
        P(("dp", "sp"), None),
        P(("dp", "sp"), None),
        P(("dp", "sp"), None),
    )
    out_specs = P(("dp", "sp"), None)
    return jax.shard_map(
        per_device, mesh=mesh, in_specs=in_specs, out_specs=out_specs, check_vma=False
    )
```

```python
import jax
import jax.numpy as jnp
from jax import lax
from jax.experimental import pallas as pl
from jax.experimental.pallas import tpu as pltpu
from jax.sharding import PartitionSpec as P

HQ = 16
KV = 4
HD = 128
BS = 64
NG = 2
LS = 8
SLOTS = 12
DOC = 4096


PAIR = 2
FAR = 1


def attention_kernel(chosen_ref, usable_ref, dense_ref, q_ref, kv_ref, o_ref, sel_ref):
    step = pl.program_id(0)
    kv_heads = kv_ref.shape[1] // (2 * HD)
    group = q_ref.shape[1] // (kv_heads * HD)
    scale = HD ** (-0.5)

    def queries(h, rows):
        return jnp.concatenate(
            [q_ref[rows, (h * group + g) * HD:(h * group + g + 1) * HD] for g in range(group)], axis=0
        )

    def finish(h, scores, values, rows):
        top = jnp.max(scores, axis=1, keepdims=True)
        expo = jnp.exp(scores - top)
        weights = (expo / jnp.sum(expo, axis=1, keepdims=True)).astype(jnp.bfloat16)
        out = jnp.dot(weights, values, preferred_element_type=jnp.float32).astype(o_ref.dtype)
        n = rows.stop - rows.start
        for g in range(group):
            col = (h * group + g) * HD
            o_ref[rows, col:col + HD] = out[g * n:(g + 1) * n]

    def scores_of(h, keys, rows):
        return lax.dot_general(
            queries(h, rows), keys, (((1,), (1,)), ((), ())), preferred_element_type=jnp.float32
        ) * scale

    def sparse_block(qb, rows):
        for j in range(SLOTS):
            start = pl.multiple_of(chosen_ref[qb * SLOTS + j] * BS, BS)
            sel_ref[j * BS:(j + 1) * BS, :] = kv_ref[pl.ds(start, BS), :]
        slot = lax.broadcasted_iota(jnp.int32, (1, SLOTS * BS), 1) // BS
        keep = jnp.zeros((1, SLOTS * BS), jnp.bool_)
        for j in range(SLOTS):
            keep = keep | ((slot == j) & (usable_ref[qb * SLOTS + j] != 0))
        for h in range(kv_heads):
            keys = sel_ref[:, h * HD:(h + 1) * HD]
            values = sel_ref[:, (kv_heads + h) * HD:(kv_heads + h + 1) * HD]
            scores = jnp.where(keep, scores_of(h, keys, rows), -1e30)
            finish(h, scores, values, rows)

    @pl.when(dense_ref[step * PAIR] != 0)
    def _():
        rows = slice(0, PAIR * BS)
        for h in range(kv_heads - FAR):
            keys = kv_ref[:, h * HD:(h + 1) * HD]
            values = kv_ref[:, (kv_heads + h) * HD:(kv_heads + h + 1) * HD]
            finish(h, scores_of(h, keys, rows), values, rows)

    @pl.when(dense_ref[step * PAIR] == 0)
    def _():
        for half in range(PAIR):
            sparse_block(step * PAIR + half, slice(half * BS, (half + 1) * BS))


def block_attention(queries2d, kv2d, chosen, usable, dense):
    rows, width = queries2d.shape
    nqb = rows // BS
    grid_spec = pltpu.PrefetchScalarGridSpec(
        num_scalar_prefetch=3,
        grid=(nqb // PAIR,),
        in_specs=[
            pl.BlockSpec((PAIR * BS, width), lambda b, *_: (b, 0)),
            pl.BlockSpec(kv2d.shape, lambda b, *_: (0, 0), pipeline_mode=pl.Buffered(1)),
        ],
        out_specs=pl.BlockSpec((PAIR * BS, width), lambda b, *_: (b, 0)),
        scratch_shapes=[pltpu.VMEM((SLOTS * BS, kv2d.shape[1]), jnp.bfloat16)],
    )
    return pl.pallas_call(
        attention_kernel,
        grid_spec=grid_spec,
        out_shape=jax.ShapeDtypeStruct(queries2d.shape, jnp.bfloat16),
        compiler_params=pltpu.CompilerParams(vmem_limit_bytes=48 * 1024 * 1024),
    )(chosen.reshape(-1), usable.reshape(-1), dense, queries2d, kv2d)


def far_kernel(q_ref, k_ref, v_ref, o_ref):
    group = q_ref.shape[1] // HD
    rows = q_ref.shape[0]
    scale = HD ** (-0.5)
    q_all = jnp.concatenate([q_ref[:, g * HD:(g + 1) * HD] for g in range(group)], axis=0)
    scores = lax.dot_general(
        q_all, k_ref[...], (((1,), (1,)), ((), ())), preferred_element_type=jnp.float32
    ) * scale
    top = jnp.max(scores, axis=1, keepdims=True)
    expo = jnp.exp(scores - top)
    weights = (expo / jnp.sum(expo, axis=1, keepdims=True)).astype(jnp.bfloat16)
    out = jnp.dot(weights, v_ref[...], preferred_element_type=jnp.float32).astype(o_ref.dtype)
    for g in range(group):
        o_ref[:, g * HD:(g + 1) * HD] = out[g * rows:(g + 1) * rows]


def far_heads(q_far, kv2d):
    doc = kv2d.shape[0]
    kv_heads = kv2d.shape[1] // (2 * HD)
    near = kv_heads - FAR
    width = q_far.shape[1] // (kv_heads - near)
    return pl.pallas_call(
        far_kernel,
        grid=(kv_heads - near,),
        in_specs=[
            pl.BlockSpec((q_far.shape[0], width), lambda i: (0, i)),
            pl.BlockSpec((doc, HD), lambda i: (0, near + i)),
            pl.BlockSpec((doc, HD), lambda i: (0, kv_heads + near + i)),
        ],
        out_specs=pl.BlockSpec((q_far.shape[0], width), lambda i: (0, i)),
        out_shape=jax.ShapeDtypeStruct(q_far.shape, jnp.bfloat16),
    )(q_far, kv2d, kv2d)


def slot_tables(block_ids, counts, first, blocks):
    nqb = block_ids.shape[0]
    query_block = first + jnp.arange(nqb, dtype=jnp.int32)
    near = query_block[:, None] + jnp.arange(-1, 2, dtype=jnp.int32)[None, :]
    near_ok = (near >= 0) & (near < blocks)
    slot_ok = jnp.arange(LS, dtype=jnp.int32)[None, :] < counts[:, None]
    pad = SLOTS - 3 - LS
    chosen = jnp.concatenate(
        [near, block_ids, jnp.broadcast_to(query_block[:, None], (nqb, pad))], axis=1
    )
    chosen = jnp.clip(chosen, 0, blocks - 1).astype(jnp.int32)
    usable = jnp.concatenate([near_ok, slot_ok, jnp.zeros((nqb, pad), jnp.bool_)], axis=1).astype(jnp.int32)
    dense = (query_block < NG).astype(jnp.int32)
    return chosen, usable, dense


def gather_rows(w):
    return lax.all_gather(w, ("dp", "sp"), axis=0, tiled=True)


def per_device(tokens, key_blocks, key_count, w_query, w_key, w_value, w_out):
    count_rows = tokens.shape[0]
    kv_cols = w_key.shape[1] + w_value.shape[1]
    q_cols = w_query.shape[1]
    weights = gather_rows(jnp.concatenate([w_key, w_value, w_query, w_out], axis=1))
    kv_sum = jnp.dot(tokens, weights[:, :kv_cols], preferred_element_type=jnp.float32)
    query_sum = jnp.dot(
        tokens, weights[:, kv_cols:kv_cols + q_cols], preferred_element_type=jnp.float32
    )
    queries = query_sum.astype(jnp.bfloat16)
    kv = kv_sum.astype(jnp.bfloat16)
    kv_all = lax.all_gather(kv, "sp", axis=0, tiled=True)
    offset = lax.axis_index("sp") * count_rows
    document = offset // DOC
    first = offset % DOC // BS
    blocks = kv_all.shape[0] // BS
    list_doc = lax.dynamic_index_in_dim(key_blocks, document, 0, keepdims=False)
    count_doc = lax.dynamic_index_in_dim(key_count, document, 0, keepdims=False)
    list_rows = lax.dynamic_slice_in_dim(list_doc, first, count_rows // BS, 0)
    count_slice = lax.dynamic_slice_in_dim(count_doc, first, count_rows // BS, 0)
    chosen, usable, dense = slot_tables(list_rows, count_slice, first, blocks)
    lead = NG * BS
    half = queries.shape[1] - FAR * (HQ // KV) * HD
    me = lax.axis_index("sp")
    q_far = lax.ppermute(queries[:lead, half:], "sp", [(0, 1)])
    out_far = lax.cond(
        me == 1, lambda: far_heads(q_far, kv_all), lambda: jnp.zeros_like(q_far)
    )
    back = lax.ppermute(out_far, "sp", [(1, 0)])
    joined = block_attention(queries, kv_all, chosen, usable, dense)
    dense_rows = jnp.concatenate([joined[:lead, :half], back], axis=1)
    head = jnp.where(me == 0, dense_rows, joined[:lead])
    joined = jnp.concatenate([head, joined[lead:]], axis=0)
    output = jnp.dot(joined, weights[:, kv_cols + q_cols:], preferred_element_type=jnp.float32)
    return output.astype(jnp.bfloat16)


def solution(mesh):
    in_specs = (
        P(("dp", "sp"), None),
        P("dp", None, None),
        P("dp", None),
        P(("dp", "sp"), None),
        P(("dp", "sp"), None),
        P(("dp", "sp"), None),
        P(("dp", "sp"), None),
    )
    out_specs = P(("dp", "sp"), None)
    return jax.shard_map(
        per_device, mesh=mesh, in_specs=in_specs, out_specs=out_specs, check_vma=False
    )
```

```python
import jax
import jax.numpy as jnp
from jax import lax
from jax.experimental import pallas as pl
from jax.experimental.pallas import tpu as pltpu
from jax.sharding import PartitionSpec as P

HQ = 16
KV = 4
HD = 128
BS = 64
NG = 2
LS = 8
SLOTS = 12
DOC = 4096


PAIR = 2
NARROW = 8
FAR = 1


def attention_kernel(chosen_ref, usable_ref, dense_ref, valid_ref, q_ref, kv_ref, o_ref, sel_ref):
    step = pl.program_id(0)
    kv_heads = kv_ref.shape[1] // (2 * HD)
    group = q_ref.shape[1] // (kv_heads * HD)
    scale = HD ** (-0.5)

    def queries(h, rows):
        return jnp.concatenate(
            [q_ref[rows, (h * group + g) * HD:(h * group + g + 1) * HD] for g in range(group)], axis=0
        )

    def finish(h, scores, values, rows):
        top = jnp.max(scores, axis=1, keepdims=True)
        expo = jnp.exp(scores - top)
        weights = (expo / jnp.sum(expo, axis=1, keepdims=True)).astype(jnp.bfloat16)
        out = jnp.dot(weights, values, preferred_element_type=jnp.float32).astype(o_ref.dtype)
        n = rows.size
        for g in range(group):
            col = (h * group + g) * HD
            o_ref[rows, col:col + HD] = out[g * n:(g + 1) * n]

    def scores_of(h, keys, rows):
        return lax.dot_general(
            queries(h, rows), keys, (((1,), (1,)), ((), ())), preferred_element_type=jnp.float32
        ) * scale

    def sparse_width(qb, rows, slots):
        for j in range(slots):
            start = pl.multiple_of(chosen_ref[qb * SLOTS + j] * BS, BS)
            sel_ref[j * BS:(j + 1) * BS, :] = kv_ref[pl.ds(start, BS), :]
        slot = lax.broadcasted_iota(jnp.int32, (1, slots * BS), 1) // BS
        keep = jnp.zeros((1, slots * BS), jnp.bool_)
        for j in range(slots):
            keep = keep | ((slot == j) & (usable_ref[qb * SLOTS + j] != 0))
        for h in range(kv_heads):
            keys = sel_ref[0:slots * BS, h * HD:(h + 1) * HD]
            values = sel_ref[0:slots * BS, (kv_heads + h) * HD:(kv_heads + h + 1) * HD]
            scores = jnp.where(keep, scores_of(h, keys, rows), -1e30)
            finish(h, scores, values, rows)

    def sparse_block(qb, rows):
        @pl.when(valid_ref[qb] <= NARROW)
        def _():
            sparse_width(qb, rows, NARROW)

        @pl.when(valid_ref[qb] > NARROW)
        def _():
            sparse_width(qb, rows, SLOTS)

    @pl.when(dense_ref[step * PAIR] != 0)
    def _():
        rows = pl.ds(0, PAIR * BS)
        for h in range(kv_heads - FAR):
            keys = kv_ref[:, h * HD:(h + 1) * HD]
            values = kv_ref[:, (kv_heads + h) * HD:(kv_heads + h + 1) * HD]
            finish(h, scores_of(h, keys, rows), values, rows)

    @pl.when(dense_ref[step * PAIR] == 0)
    def _():
        def body(half, carry):
            sparse_block(step * PAIR + half, pl.ds(pl.multiple_of(half * BS, BS), BS))
            return carry

        lax.fori_loop(0, PAIR, body, 0)


def block_attention(queries2d, kv2d, chosen, usable, dense, valid):
    rows, width = queries2d.shape
    nqb = rows // BS
    grid_spec = pltpu.PrefetchScalarGridSpec(
        num_scalar_prefetch=4,
        grid=(nqb // PAIR,),
        in_specs=[
            pl.BlockSpec((PAIR * BS, width), lambda b, *_: (b, 0)),
            pl.BlockSpec(kv2d.shape, lambda b, *_: (0, 0), pipeline_mode=pl.Buffered(1)),
        ],
        out_specs=pl.BlockSpec((PAIR * BS, width), lambda b, *_: (b, 0)),
        scratch_shapes=[pltpu.VMEM((SLOTS * BS, kv2d.shape[1]), jnp.bfloat16)],
    )
    return pl.pallas_call(
        attention_kernel,
        grid_spec=grid_spec,
        out_shape=jax.ShapeDtypeStruct(queries2d.shape, jnp.bfloat16),
        compiler_params=pltpu.CompilerParams(vmem_limit_bytes=48 * 1024 * 1024),
    )(chosen.reshape(-1), usable.reshape(-1), dense, valid, queries2d, kv2d)


def far_kernel(q_ref, k_ref, v_ref, o_ref):
    group = q_ref.shape[1] // HD
    rows = q_ref.shape[0]
    scale = HD ** (-0.5)
    q_all = jnp.concatenate([q_ref[:, g * HD:(g + 1) * HD] for g in range(group)], axis=0)
    scores = lax.dot_general(
        q_all, k_ref[...], (((1,), (1,)), ((), ())), preferred_element_type=jnp.float32
    ) * scale
    top = jnp.max(scores, axis=1, keepdims=True)
    expo = jnp.exp(scores - top)
    weights = (expo / jnp.sum(expo, axis=1, keepdims=True)).astype(jnp.bfloat16)
    out = jnp.dot(weights, v_ref[...], preferred_element_type=jnp.float32).astype(o_ref.dtype)
    for g in range(group):
        o_ref[:, g * HD:(g + 1) * HD] = out[g * rows:(g + 1) * rows]


def far_heads(q_far, kv2d):
    doc = kv2d.shape[0]
    kv_heads = kv2d.shape[1] // (2 * HD)
    near = kv_heads - FAR
    width = q_far.shape[1] // (kv_heads - near)
    return pl.pallas_call(
        far_kernel,
        grid=(kv_heads - near,),
        in_specs=[
            pl.BlockSpec((q_far.shape[0], width), lambda i: (0, i)),
            pl.BlockSpec((doc, HD), lambda i: (0, near + i)),
            pl.BlockSpec((doc, HD), lambda i: (0, kv_heads + near + i)),
        ],
        out_specs=pl.BlockSpec((q_far.shape[0], width), lambda i: (0, i)),
        out_shape=jax.ShapeDtypeStruct(q_far.shape, jnp.bfloat16),
    )(q_far, kv2d, kv2d)


def slot_tables(block_ids, counts, first, blocks):
    nqb = block_ids.shape[0]
    query_block = first + jnp.arange(nqb, dtype=jnp.int32)
    near = query_block[:, None] + jnp.arange(-1, 2, dtype=jnp.int32)[None, :]
    near_ok = (near >= 0) & (near < blocks)
    slot_ok = jnp.arange(LS, dtype=jnp.int32)[None, :] < counts[:, None]
    pad = SLOTS - 3 - LS
    chosen = jnp.concatenate(
        [near, block_ids, jnp.broadcast_to(query_block[:, None], (nqb, pad))], axis=1
    )
    chosen = jnp.clip(chosen, 0, blocks - 1).astype(jnp.int32)
    usable = jnp.concatenate([near_ok, slot_ok, jnp.zeros((nqb, pad), jnp.bool_)], axis=1).astype(jnp.int32)
    dense = (query_block < NG).astype(jnp.int32)
    order = jnp.argsort(1 - usable, axis=1, stable=True)
    chosen = jnp.take_along_axis(chosen, order, axis=1)
    usable = jnp.take_along_axis(usable, order, axis=1)
    valid = jnp.sum(usable, axis=1).astype(jnp.int32)
    return chosen, usable, dense, valid


def gather_rows(w):
    return lax.all_gather(w, ("dp", "sp"), axis=0, tiled=True)


def per_device(tokens, key_blocks, key_count, w_query, w_key, w_value, w_out):
    count_rows = tokens.shape[0]
    kv_cols = w_key.shape[1] + w_value.shape[1]
    q_cols = w_query.shape[1]
    weights = gather_rows(jnp.concatenate([w_key, w_value, w_query, w_out], axis=1))
    kv_sum = jnp.dot(tokens, weights[:, :kv_cols], preferred_element_type=jnp.float32)
    query_sum = jnp.dot(
        tokens, weights[:, kv_cols:kv_cols + q_cols], preferred_element_type=jnp.float32
    )
    queries = query_sum.astype(jnp.bfloat16)
    kv = kv_sum.astype(jnp.bfloat16)
    kv_all = lax.all_gather(kv, "sp", axis=0, tiled=True)
    offset = lax.axis_index("sp") * count_rows
    document = offset // DOC
    first = offset % DOC // BS
    blocks = kv_all.shape[0] // BS
    list_doc = lax.dynamic_index_in_dim(key_blocks, document, 0, keepdims=False)
    count_doc = lax.dynamic_index_in_dim(key_count, document, 0, keepdims=False)
    list_rows = lax.dynamic_slice_in_dim(list_doc, first, count_rows // BS, 0)
    count_slice = lax.dynamic_slice_in_dim(count_doc, first, count_rows // BS, 0)
    chosen, usable, dense, valid = slot_tables(list_rows, count_slice, first, blocks)
    lead = NG * BS
    half = queries.shape[1] - FAR * (HQ // KV) * HD
    me = lax.axis_index("sp")
    q_far = lax.ppermute(queries[:lead, half:], "sp", [(0, 1)])
    out_far = lax.cond(
        me == 1, lambda: far_heads(q_far, kv_all), lambda: jnp.zeros_like(q_far)
    )
    back = lax.ppermute(out_far, "sp", [(1, 0)])
    joined = block_attention(queries, kv_all, chosen, usable, dense, valid)
    dense_rows = jnp.concatenate([joined[:lead, :half], back], axis=1)
    head = jnp.where(me == 0, dense_rows, joined[:lead])
    joined = jnp.concatenate([head, joined[lead:]], axis=0)
    output = jnp.dot(joined, weights[:, kv_cols + q_cols:], preferred_element_type=jnp.float32)
    return output.astype(jnp.bfloat16)


def solution(mesh):
    in_specs = (
        P(("dp", "sp"), None),
        P("dp", None, None),
        P("dp", None),
        P(("dp", "sp"), None),
        P(("dp", "sp"), None),
        P(("dp", "sp"), None),
        P(("dp", "sp"), None),
    )
    out_specs = P(("dp", "sp"), None)
    return jax.shard_map(
        per_device, mesh=mesh, in_specs=in_specs, out_specs=out_specs, check_vma=False
    )
```

```python
import jax
import jax.numpy as jnp
from jax import lax
from jax.experimental import pallas as pl
from jax.experimental.pallas import tpu as pltpu
from jax.sharding import PartitionSpec as P

HQ = 16
KV = 4
HD = 128
BS = 64
NG = 2
LS = 8
SLOTS = 12
DOC = 4096


PAIR = 2
NARROW = 8
MIDDLE = 10
FAR = 1


def attention_kernel(chosen_ref, usable_ref, dense_ref, valid_ref, q_ref, kv_ref, o_ref, sel_ref):
    step = pl.program_id(0)
    kv_heads = kv_ref.shape[1] // (2 * HD)
    group = q_ref.shape[1] // (kv_heads * HD)
    scale = HD ** (-0.5)

    def queries(h, rows):
        return jnp.concatenate(
            [q_ref[rows, (h * group + g) * HD:(h * group + g + 1) * HD] for g in range(group)], axis=0
        )

    def finish(h, scores, values, rows):
        top = jnp.max(scores, axis=1, keepdims=True)
        expo = jnp.exp(scores - top)
        weights = (expo / jnp.sum(expo, axis=1, keepdims=True)).astype(jnp.bfloat16)
        out = jnp.dot(weights, values, preferred_element_type=jnp.float32).astype(o_ref.dtype)
        n = rows.size
        for g in range(group):
            col = (h * group + g) * HD
            o_ref[rows, col:col + HD] = out[g * n:(g + 1) * n]

    def scores_of(h, keys, rows):
        return lax.dot_general(
            queries(h, rows), keys, (((1,), (1,)), ((), ())), preferred_element_type=jnp.float32
        ) * scale

    def sparse_width(qb, rows, slots):
        for j in range(slots):
            start = pl.multiple_of(chosen_ref[qb * SLOTS + j] * BS, BS)
            sel_ref[j * BS:(j + 1) * BS, :] = kv_ref[pl.ds(start, BS), :]
        slot = lax.broadcasted_iota(jnp.int32, (1, slots * BS), 1) // BS
        keep = jnp.zeros((1, slots * BS), jnp.bool_)
        for j in range(slots):
            keep = keep | ((slot == j) & (usable_ref[qb * SLOTS + j] != 0))
        for h in range(kv_heads):
            keys = sel_ref[0:slots * BS, h * HD:(h + 1) * HD]
            values = sel_ref[0:slots * BS, (kv_heads + h) * HD:(kv_heads + h + 1) * HD]
            scores = jnp.where(keep, scores_of(h, keys, rows), -1e30)
            finish(h, scores, values, rows)

    def sparse_block(qb, rows):
        @pl.when(valid_ref[qb] <= NARROW)
        def _():
            sparse_width(qb, rows, NARROW)

        @pl.when((valid_ref[qb] > NARROW) & (valid_ref[qb] <= MIDDLE))
        def _():
            sparse_width(qb, rows, MIDDLE)

        @pl.when(valid_ref[qb] > MIDDLE)
        def _():
            sparse_width(qb, rows, SLOTS)

    @pl.when(dense_ref[step * PAIR] != 0)
    def _():
        rows = pl.ds(0, PAIR * BS)
        for h in range(kv_heads - FAR):
            keys = kv_ref[:, h * HD:(h + 1) * HD]
            values = kv_ref[:, (kv_heads + h) * HD:(kv_heads + h + 1) * HD]
            finish(h, scores_of(h, keys, rows), values, rows)

    @pl.when(dense_ref[step * PAIR] == 0)
    def _():
        def body(half, carry):
            sparse_block(step * PAIR + half, pl.ds(pl.multiple_of(half * BS, BS), BS))
            return carry

        lax.fori_loop(0, PAIR, body, 0)


def block_attention(queries2d, kv2d, chosen, usable, dense, valid):
    rows, width = queries2d.shape
    nqb = rows // BS
    grid_spec = pltpu.PrefetchScalarGridSpec(
        num_scalar_prefetch=4,
        grid=(nqb // PAIR,),
        in_specs=[
            pl.BlockSpec((PAIR * BS, width), lambda b, *_: (b, 0)),
            pl.BlockSpec(kv2d.shape, lambda b, *_: (0, 0), pipeline_mode=pl.Buffered(1)),
        ],
        out_specs=pl.BlockSpec((PAIR * BS, width), lambda b, *_: (b, 0)),
        scratch_shapes=[pltpu.VMEM((SLOTS * BS, kv2d.shape[1]), jnp.bfloat16)],
    )
    return pl.pallas_call(
        attention_kernel,
        grid_spec=grid_spec,
        out_shape=jax.ShapeDtypeStruct(queries2d.shape, jnp.bfloat16),
        compiler_params=pltpu.CompilerParams(vmem_limit_bytes=48 * 1024 * 1024),
    )(chosen.reshape(-1), usable.reshape(-1), dense, valid, queries2d, kv2d)


def far_kernel(q_ref, k_ref, v_ref, o_ref):
    group = q_ref.shape[1] // HD
    rows = q_ref.shape[0]
    scale = HD ** (-0.5)
    q_all = jnp.concatenate([q_ref[:, g * HD:(g + 1) * HD] for g in range(group)], axis=0)
    scores = lax.dot_general(
        q_all, k_ref[...], (((1,), (1,)), ((), ())), preferred_element_type=jnp.float32
    ) * scale
    top = jnp.max(scores, axis=1, keepdims=True)
    expo = jnp.exp(scores - top)
    weights = (expo / jnp.sum(expo, axis=1, keepdims=True)).astype(jnp.bfloat16)
    out = jnp.dot(weights, v_ref[...], preferred_element_type=jnp.float32).astype(o_ref.dtype)
    for g in range(group):
        o_ref[:, g * HD:(g + 1) * HD] = out[g * rows:(g + 1) * rows]


def far_heads(q_far, kv2d):
    doc = kv2d.shape[0]
    kv_heads = kv2d.shape[1] // (2 * HD)
    near = kv_heads - FAR
    width = q_far.shape[1] // (kv_heads - near)
    return pl.pallas_call(
        far_kernel,
        grid=(kv_heads - near,),
        in_specs=[
            pl.BlockSpec((q_far.shape[0], width), lambda i: (0, i)),
            pl.BlockSpec((doc, HD), lambda i: (0, near + i)),
            pl.BlockSpec((doc, HD), lambda i: (0, kv_heads + near + i)),
        ],
        out_specs=pl.BlockSpec((q_far.shape[0], width), lambda i: (0, i)),
        out_shape=jax.ShapeDtypeStruct(q_far.shape, jnp.bfloat16),
    )(q_far, kv2d, kv2d)


def slot_tables(block_ids, counts, first, blocks):
    nqb = block_ids.shape[0]
    query_block = first + jnp.arange(nqb, dtype=jnp.int32)
    near = query_block[:, None] + jnp.arange(-1, 2, dtype=jnp.int32)[None, :]
    near_ok = (near >= 0) & (near < blocks)
    slot_ok = jnp.arange(LS, dtype=jnp.int32)[None, :] < counts[:, None]
    pad = SLOTS - 3 - LS
    chosen = jnp.concatenate(
        [near, block_ids, jnp.broadcast_to(query_block[:, None], (nqb, pad))], axis=1
    )
    chosen = jnp.clip(chosen, 0, blocks - 1).astype(jnp.int32)
    usable = jnp.concatenate([near_ok, slot_ok, jnp.zeros((nqb, pad), jnp.bool_)], axis=1).astype(jnp.int32)
    dense = (query_block < NG).astype(jnp.int32)
    order = jnp.argsort(1 - usable, axis=1, stable=True)
    chosen = jnp.take_along_axis(chosen, order, axis=1)
    usable = jnp.take_along_axis(usable, order, axis=1)
    valid = jnp.sum(usable, axis=1).astype(jnp.int32)
    return chosen, usable, dense, valid


def gather_rows(w):
    return lax.all_gather(w, ("dp", "sp"), axis=0, tiled=True)


def per_device(tokens, key_blocks, key_count, w_query, w_key, w_value, w_out):
    count_rows = tokens.shape[0]
    kv_cols = w_key.shape[1] + w_value.shape[1]
    q_cols = w_query.shape[1]
    weights = gather_rows(jnp.concatenate([w_key, w_value, w_query, w_out], axis=1))
    kv_sum = jnp.dot(tokens, weights[:, :kv_cols], preferred_element_type=jnp.float32)
    query_sum = jnp.dot(
        tokens, weights[:, kv_cols:kv_cols + q_cols], preferred_element_type=jnp.float32
    )
    queries = query_sum.astype(jnp.bfloat16)
    kv = kv_sum.astype(jnp.bfloat16)
    kv_all = lax.all_gather(kv, "sp", axis=0, tiled=True)
    offset = lax.axis_index("sp") * count_rows
    document = offset // DOC
    first = offset % DOC // BS
    blocks = kv_all.shape[0] // BS
    list_doc = lax.dynamic_index_in_dim(key_blocks, document, 0, keepdims=False)
    count_doc = lax.dynamic_index_in_dim(key_count, document, 0, keepdims=False)
    list_rows = lax.dynamic_slice_in_dim(list_doc, first, count_rows // BS, 0)
    count_slice = lax.dynamic_slice_in_dim(count_doc, first, count_rows // BS, 0)
    chosen, usable, dense, valid = slot_tables(list_rows, count_slice, first, blocks)
    lead = NG * BS
    half = queries.shape[1] - FAR * (HQ // KV) * HD
    me = lax.axis_index("sp")
    q_far = lax.ppermute(queries[:lead, half:], "sp", [(0, 1)])
    out_far = lax.cond(
        me == 1, lambda: far_heads(q_far, kv_all), lambda: jnp.zeros_like(q_far)
    )
    back = lax.ppermute(out_far, "sp", [(1, 0)])
    joined = block_attention(queries, kv_all, chosen, usable, dense, valid)
    dense_rows = jnp.concatenate([joined[:lead, :half], back], axis=1)
    head = jnp.where(me == 0, dense_rows, joined[:lead])
    joined = jnp.concatenate([head, joined[lead:]], axis=0)
    output = jnp.dot(joined, weights[:, kv_cols + q_cols:], preferred_element_type=jnp.float32)
    return output.astype(jnp.bfloat16)


def solution(mesh):
    in_specs = (
        P(("dp", "sp"), None),
        P("dp", None, None),
        P("dp", None),
        P(("dp", "sp"), None),
        P(("dp", "sp"), None),
        P(("dp", "sp"), None),
        P(("dp", "sp"), None),
    )
    out_specs = P(("dp", "sp"), None)
    return jax.shard_map(
        per_device, mesh=mesh, in_specs=in_specs, out_specs=out_specs, check_vma=False
    )
```
